256 devices in a mesh: section: 4 (over z_lo, core), dp: 64 (over y, x, z_hi).
Axes of the slice: x: 4, y: 4, z: 8 (z_hi: 4, z_lo: 2; z = z_hi * 2 + z_lo), core: 2. Of those that a mesh axis runs over, the one named last changes fastest.
Arguments:
- activations_in: bfloat16 [2, 4096, 8192], P(None, 'dp'), may hold values from -6 to 6
- cotangent: bfloat16 [2, 4096, 8192], P(None, 'dp'), may hold values from -6 to 6
- value_tiles: bfloat16 [4, 128, 128, 128], P('section'), may hold values from -0.0625 to 0.0625
- value_ids: int32 [4, 128], P('section'), may hold values from 0 to 255, as said below
- out_tiles: bfloat16 [4, 192, 128, 128], P('section', 'dp'), may hold values from -0.25 to 0.25
- out_ids: int32 [4, 192], P('section'), may hold values from 0 to 255, as said below
- out_count: int32 [4, 64], P('section'), may hold values from 1 to 3, as said below
Outputs:
- section_outputs: bfloat16 [4, 2, 4096, 8192], P('section', None, 'dp')
- input_grads: bfloat16 [4, 2, 4096, 8192], P('section', None, 'dp')
- out_grad: float32 [4, 192, 128, 128], P('section', 'dp')
The draws below stay inside these ranges and needn't reach their ends.
Inputs may be any that keep to these rules, and one draw needn't show every extreme that they name: `value_ids`: for each layer, 128 different tile numbers. `out_ids`: for each layer, 192 different tile numbers; slot g lies on index g // 3 of dp. The live slots of an index of dp are its first out_count slots; in each layer some index has all 3 slots live.
All inputs are finite; a program needn't handle non-finite values.
Results may differ from the reference program's by a relative error of at most 0.008.
Values may be sent and summed in bfloat16 or wider, within the bound.
No kernel may reach another device: no remote copies, remote signals or barrier semaphores. Data moves between devices by JAX's collectives and lax.ppermute only.
A program may use at most 192 MiB of HBM per device.

```python
import math
import jax
import jax.numpy as jnp

D = 8192
VW = 512
TILE = 128
MB = 2
TOKENS = 4096
ALLTILES = 256
TPS = 3
SLOTS = 192
VSLOTS = 128
N_SECTION = 4
N_DP = 64


def draw_value_ids(key, part):
    section_keys = jax.random.split(jax.random.fold_in(key, 11), N_SECTION)

    def pick_tiles(sub_key):
        return jax.random.permutation(sub_key, ALLTILES)[:VSLOTS]
    return jax.vmap(pick_tiles)(section_keys).astype(jnp.int32)


def draw_out_ids(key, part):
    section_keys = jax.random.split(jax.random.fold_in(key, 12), N_SECTION)

    def pick_tiles(sub_key):
        return jax.random.permutation(sub_key, ALLTILES)[:SLOTS]
    return jax.vmap(pick_tiles)(section_keys).astype(jnp.int32)


def draw_out_count(key, part):
    base_count = jax.random.randint(jax.random.fold_in(key, 13), (N_SECTION, N_DP), TPS // 3, TPS + 1)
    fullest = jax.random.randint(jax.random.fold_in(key, 14), (N_SECTION, 1), 0, N_DP)
    marked = jnp.arange(N_DP)[None, :] == fullest
    return jnp.where(marked, TPS, base_count).astype(jnp.int32)


def block_levels(stream_key, dims, cuts, smallest, top_value):
    loudness, own = 1.0, jax.random.fold_in(stream_key, 6)
    for position, blocks in cuts:
        draws = jnp.exp(jax.random.uniform(jax.random.fold_in(own, position), (blocks,), jnp.float32, smallest / len(cuts), top_value / len(cuts)))
        loudness = loudness * jnp.repeat(draws, dims[position] // blocks).reshape([-1 if axis == position else 1 for axis in range(len(dims))])
    return loudness


def scatter_about(own_key, extent, width, limit, cuts=(), held_as=jnp.bfloat16):
    values = width * jax.random.normal(own_key, extent, jnp.float32)
    if cuts:
        values = values * block_levels(own_key, extent, cuts, -0.22, 0.18)
    return jnp.clip(values, -limit, limit).astype(held_as)


def setup_inputs(seed: int = 0) -> dict:
    arg_keys = jax.random.split(jax.random.key(seed), 8)
    activations_in = scatter_about(arg_keys[0], (MB, TOKENS, D), 1.0, 6.0, ((1, 64),))
    cotangent = scatter_about(arg_keys[1], (MB, TOKENS, D), 1.0, 6.0, ((1, 64),))
    value_tiles = scatter_about(arg_keys[2], (N_SECTION, VSLOTS, TILE, TILE), D ** -0.5, 0.0625, ((0, 4),))
    value_ids = draw_value_ids(jax.random.fold_in(arg_keys[7], 71), 0)
    out_tiles = scatter_about(arg_keys[4], (N_SECTION, SLOTS, TILE, TILE), VW ** -0.5, 0.25, ((0, 4), (1, 64)))
    out_ids = draw_out_ids(jax.random.fold_in(arg_keys[7], 71), 0)
    out_count = draw_out_count(jax.random.fold_in(arg_keys[7], 71), 0)
    return dict(activations_in=activations_in, cotangent=cotangent, value_tiles=value_tiles, value_ids=value_ids, out_tiles=out_tiles, out_ids=out_ids, out_count=out_count)


def tile_grid(tile_data, tile_ids, row_blocks, col_blocks):
    grid = jnp.zeros((row_blocks * col_blocks, TILE, TILE), jnp.float32)
    grid = grid.at[tile_ids.astype(jnp.int32)].set(tile_data.astype(jnp.float32))
    grid = grid.reshape(row_blocks, col_blocks, TILE, TILE).transpose(0, 2, 1, 3)
    return grid.reshape(row_blocks * TILE, col_blocks * TILE).astype(jnp.bfloat16)

def live_slots(count_row):
    return (jnp.arange(TPS, dtype=jnp.int32)[None, :] < count_row[:, None]).reshape(-1)

def reference(activations_in, cotangent, value_tiles, value_ids, out_tiles, out_ids, out_count):
    value_blocks = VW // TILE
    model_blocks = D // TILE
    grad_scale = 1.0 / math.sqrt(MB * TOKENS)
    value_mats = []
    out_mats = []
    live_list = []
    for section_index in range(N_SECTION):
        value_mats.append(tile_grid(value_tiles[section_index], value_ids[section_index], model_blocks, value_blocks))
        live_mask = live_slots(out_count[section_index])
        masked = jnp.where(live_mask[:, None, None], out_tiles[section_index], jnp.zeros_like(out_tiles[section_index]))
        out_mats.append(tile_grid(masked, out_ids[section_index], value_blocks, model_blocks))
        live_list.append(live_mask)
    hidden = activations_in
    values = []
    outputs = []
    for section_index in range(N_SECTION):
        value_rows = jnp.dot(hidden, value_mats[section_index], preferred_element_type=jnp.float32).astype(jnp.bfloat16)
        update = jnp.dot(value_rows, out_mats[section_index], preferred_element_type=jnp.float32)
        hidden = (hidden.astype(jnp.float32) + update).astype(jnp.bfloat16)
        values.append(value_rows)
        outputs.append(hidden)
    grad_rows = cotangent
    input_grads = [None] * N_SECTION
    out_grads = [None] * N_SECTION
    for section_index in reversed(range(N_SECTION)):
        grad_values = jnp.dot(grad_rows, out_mats[section_index].T, preferred_element_type=jnp.float32).astype(jnp.bfloat16)
        weight_grad = jnp.dot(values[section_index].reshape(-1, VW).T, grad_rows.reshape(-1, D), preferred_element_type=jnp.float32) * grad_scale
        tiled = weight_grad.reshape(value_blocks, TILE, model_blocks, TILE).transpose(0, 2, 1, 3).reshape(value_blocks * model_blocks, TILE, TILE)
        picked = tiled[out_ids[section_index].astype(jnp.int32)]
        out_grads[section_index] = jnp.where(live_list[section_index][:, None, None], picked, jnp.zeros_like(picked))
        extra_term = jnp.dot(grad_values, value_mats[section_index].T, preferred_element_type=jnp.float32)
        grad_rows = (grad_rows.astype(jnp.float32) + extra_term).astype(jnp.bfloat16)
        input_grads[section_index] = grad_rows
    return (jnp.stack(outputs), jnp.stack(input_grads), jnp.stack(out_grads))
```

```python
import math

import jax
import jax.numpy as jnp
from jax import lax
from jax.sharding import PartitionSpec as P

VW = 512


def dense_from_tiles(selector, tiles, row_blocks, col_blocks):
    tile_width = tiles.shape[-1]
    grid = jnp.einsum(
        "rck,kij->ricj",
        selector.reshape(row_blocks, col_blocks, -1),
        tiles,
        preferred_element_type=jnp.float32,
    ).astype(jnp.bfloat16)
    return grid.reshape(row_blocks * tile_width, col_blocks * tile_width)


def on_device(activations_in, cotangent, value_tiles, value_ids, out_tiles, out_ids, out_count):
    section_index = lax.axis_index("section")
    section_count = lax.axis_size("section")
    shard_count = lax.axis_size("dp")
    shard_index = lax.axis_index("dp")
    micro_count = activations_in.shape[0]
    tok_rows = activations_in.shape[1]
    model_width = activations_in.shape[2]
    all_rows = micro_count * tok_rows
    tile_width = value_tiles.shape[-1]
    value_width = VW
    value_blocks = value_width // tile_width
    model_blocks = model_width // tile_width
    slot_share = out_tiles.shape[1]
    out_slot = out_ids[0]
    live_mask = (jnp.arange(slot_share, dtype=jnp.int32)[None, :] < out_count[0][:, None]).reshape(
        -1
    )
    own_live = lax.dynamic_slice_in_dim(live_mask, shard_index * slot_share, slot_share)
    gathered = lax.all_gather(out_tiles[0], "dp", axis=0, tiled=True)

    tile_numbers = jnp.arange(value_blocks * model_blocks, dtype=jnp.int32)
    value_select = (value_ids[0][None, :] == tile_numbers[:, None]).astype(jnp.bfloat16)
    value_w = dense_from_tiles(value_select, value_tiles[0], model_blocks, value_blocks)
    out_select = (
        (out_slot[None, :] == tile_numbers[:, None]) & live_mask[None, :]
    ).astype(jnp.bfloat16)
    out_w = dense_from_tiles(out_select, gathered, value_blocks, model_blocks)

    def forward_layer(hidden):
        value_rows = jnp.dot(hidden, value_w, preferred_element_type=jnp.float32).astype(
            jnp.bfloat16
        )
        update = jnp.dot(value_rows, out_w, preferred_element_type=jnp.float32)
        result = (hidden.astype(jnp.float32) + update).astype(jnp.bfloat16)
        return value_rows, result

    def backward_layer(grad_rows):
        grad_values = lax.dot_general(
            grad_rows, out_w, (((1,), (1,)), ((), ())), preferred_element_type=jnp.float32
        ).astype(jnp.bfloat16)
        extra_term = lax.dot_general(
            grad_values, value_w, (((1,), (1,)), ((), ())), preferred_element_type=jnp.float32
        )
        return (grad_rows.astype(jnp.float32) + extra_term).astype(jnp.bfloat16)

    first_input = activations_in.reshape(all_rows, model_width)
    last_grad = cotangent.reshape(all_rows, model_width)
    value_store = jnp.zeros((all_rows, value_width), jnp.bfloat16)
    act_store = jnp.zeros((all_rows, model_width), jnp.bfloat16)
    input_store = jnp.zeros((all_rows, model_width), jnp.bfloat16)
    used_grad = jnp.zeros((all_rows, model_width), jnp.bfloat16)
    forward_in = first_input
    backward_in = last_grad
    for step_number in range(section_count):
        back_section = section_count - 1 - step_number
        value_store, act_store = lax.cond(
            section_index == step_number,
            lambda ops: forward_layer(ops[0]),
            lambda ops: (ops[1], ops[2]),
            (forward_in, value_store, act_store),
        )
        input_store, used_grad = lax.cond(
            section_index == back_section,
            lambda ops: (backward_layer(ops[0]), ops[0]),
            lambda ops: (ops[1], ops[2]),
            (backward_in, input_store, used_grad),
        )
        if step_number + 1 < section_count:
            forward_in = lax.ppermute(act_store, "section", [(step_number, step_number + 1)])
            backward_in = lax.ppermute(
                input_store, "section", [(back_section, back_section - 1)]
            )

    grad_scale = 1.0 / math.sqrt(micro_count * tok_rows * shard_count)
    weight_tiles = jnp.einsum(
        "tri,tcj->rcij",
        value_store.reshape(all_rows, value_blocks, tile_width),
        used_grad.reshape(all_rows, model_blocks, tile_width),
        preferred_element_type=jnp.float32,
    ).astype(jnp.bfloat16)
    weight_tiles = weight_tiles.reshape(value_blocks * model_blocks, tile_width, tile_width)
    picked = jnp.take(weight_tiles, out_slot, axis=0)
    received = lax.all_to_all(
        picked.reshape(shard_count, slot_share, tile_width, tile_width), "dp", 0, 0, tiled=True
    )
    summed = received.astype(jnp.float32).sum(axis=0)
    scaled = summed * grad_scale
    out_grad = jnp.where(own_live[:, None, None], scaled, jnp.zeros_like(scaled))
    section_out = act_store.reshape(micro_count, tok_rows, model_width)
    grad_out = input_store.reshape(micro_count, tok_rows, model_width)
    return (section_out[None], grad_out[None], out_grad[None])


def solution(mesh):
    in_specs = (
        P(None, "dp", None),
        P(None, "dp", None),
        P("section", None, None, None),
        P("section", None),
        P("section", "dp", None, None),
        P("section", None),
        P("section", None),
    )
    out_specs = (
        P("section", None, "dp", None),
        P("section", None, "dp", None),
        P("section", "dp", None, None),
    )
    return jax.shard_map(
        on_device, mesh=mesh, in_specs=in_specs, out_specs=out_specs, check_vma=False
    )
```

```python
import math

import jax
import jax.numpy as jnp
from jax import lax
from jax.experimental import pallas as pl
from jax.experimental.pallas import tpu as pltpu
from jax.sharding import PartitionSpec as P

VW = 512
INTERPRET = False


def place_tiles(source, tiles, row_blocks, col_blocks, rows_per_step):
    tile_width = tiles.shape[-1]

    def kernel(source_ref, tiles_ref, out_ref):
        step = pl.program_id(0)
        for row in range(rows_per_step):
            for col in range(col_blocks):
                pick = source_ref[(step * rows_per_step + row) * col_blocks + col]
                tile = tiles_ref[jnp.maximum(pick, 0)]
                tile = jnp.where(pick >= 0, tile, jnp.zeros_like(tile))
                out_ref[
                    row * tile_width : (row + 1) * tile_width,
                    col * tile_width : (col + 1) * tile_width,
                ] = tile

    grid_spec = pltpu.PrefetchScalarGridSpec(
        num_scalar_prefetch=1,
        grid=(row_blocks // rows_per_step,),
        in_specs=[pl.BlockSpec(tiles.shape, lambda step, src: (0, 0, 0))],
        out_specs=pl.BlockSpec(
            (rows_per_step * tile_width, col_blocks * tile_width), lambda step, src: (step, 0)
        ),
    )
    return pl.pallas_call(
        kernel,
        grid_spec=grid_spec,
        out_shape=jax.ShapeDtypeStruct(
            (row_blocks * tile_width, col_blocks * tile_width), tiles.dtype
        ),
        interpret=INTERPRET,
    )(source, tiles)


def tile_products(tile_ids, left_t, right, col_blocks, slots_per_step):
    slot_count = tile_ids.shape[0]
    tile_width = right.shape[-1]

    def kernel(ids_ref, left_ref, right_ref, out_ref):
        step = pl.program_id(0)
        for slot in range(slots_per_step):
            tile = ids_ref[step * slots_per_step + slot]
            out_ref[slot] = jnp.dot(
                left_ref[tile // col_blocks],
                right_ref[tile % col_blocks],
                preferred_element_type=jnp.float32,
            )

    grid_spec = pltpu.PrefetchScalarGridSpec(
        num_scalar_prefetch=1,
        grid=(slot_count // slots_per_step,),
        in_specs=[
            pl.BlockSpec(left_t.shape, lambda step, ids: (0, 0, 0)),
            pl.BlockSpec(right.shape, lambda step, ids: (0, 0, 0)),
        ],
        out_specs=pl.BlockSpec(
            (slots_per_step, tile_width, tile_width), lambda step, ids: (step, 0, 0)
        ),
    )
    return pl.pallas_call(
        kernel,
        grid_spec=grid_spec,
        out_shape=jax.ShapeDtypeStruct((slot_count, tile_width, tile_width), jnp.float32),
        interpret=INTERPRET,
    )(tile_ids, left_t, right)


def on_device(activations_in, cotangent, value_tiles, value_ids, out_tiles, out_ids, out_count):
    section_index = lax.axis_index("section")
    section_count = lax.axis_size("section")
    shard_count = lax.axis_size("dp")
    shard_index = lax.axis_index("dp")
    micro_count = activations_in.shape[0]
    tok_rows = activations_in.shape[1]
    model_width = activations_in.shape[2]
    all_rows = micro_count * tok_rows
    tile_width = value_tiles.shape[-1]
    value_width = VW
    value_blocks = value_width // tile_width
    model_blocks = model_width // tile_width
    slot_share = out_tiles.shape[1]
    out_slot = out_ids[0]
    live_mask = (jnp.arange(slot_share, dtype=jnp.int32)[None, :] < out_count[0][:, None]).reshape(
        -1
    )
    own_live = lax.dynamic_slice_in_dim(live_mask, shard_index * slot_share, slot_share)
    gathered = lax.all_gather(out_tiles[0], "dp", axis=0, tiled=True)

    tile_numbers = jnp.arange(value_blocks * model_blocks, dtype=jnp.int32)
    value_order = jnp.arange(value_ids.shape[1], dtype=jnp.int32)
    value_source = jnp.max(
        jnp.where(value_ids[0][None, :] == tile_numbers[:, None], value_order[None, :], -1), axis=1
    )
    value_w = place_tiles(value_source, value_tiles[0], model_blocks, value_blocks, 8)
    slot_order = jnp.arange(out_slot.shape[0], dtype=jnp.int32)
    out_source = jnp.max(
        jnp.where(
            (out_slot[None, :] == tile_numbers[:, None]) & live_mask[None, :],
            slot_order[None, :],
            -1,
        ),
        axis=1,
    )
    out_w = place_tiles(out_source, gathered, value_blocks, model_blocks, 1)

    def forward_layer(hidden):
        value_rows = jnp.dot(hidden, value_w, preferred_element_type=jnp.float32).astype(
            jnp.bfloat16
        )
        update = jnp.dot(value_rows, out_w, preferred_element_type=jnp.float32)
        result = (hidden.astype(jnp.float32) + update).astype(jnp.bfloat16)
        return value_rows, result

    def backward_layer(grad_rows):
        grad_values = lax.dot_general(
            grad_rows, out_w, (((1,), (1,)), ((), ())), preferred_element_type=jnp.float32
        ).astype(jnp.bfloat16)
        extra_term = lax.dot_general(
            grad_values, value_w, (((1,), (1,)), ((), ())), preferred_element_type=jnp.float32
        )
        return (grad_rows.astype(jnp.float32) + extra_term).astype(jnp.bfloat16)

    first_input = activations_in.reshape(all_rows, model_width)
    last_grad = cotangent.reshape(all_rows, model_width)
    value_store = jnp.zeros((all_rows, value_width), jnp.bfloat16)
    act_store = jnp.zeros((all_rows, model_width), jnp.bfloat16)
    input_store = jnp.zeros((all_rows, model_width), jnp.bfloat16)
    used_grad = jnp.zeros((all_rows, model_width), jnp.bfloat16)
    forward_in = first_input
    backward_in = last_grad
    for step_number in range(section_count):
        back_section = section_count - 1 - step_number
        value_store, act_store = lax.cond(
            section_index == step_number,
            lambda ops: forward_layer(ops[0]),
            lambda ops: (ops[1], ops[2]),
            (forward_in, value_store, act_store),
        )
        input_store, used_grad = lax.cond(
            section_index == back_section,
            lambda ops: (backward_layer(ops[0]), ops[0]),
            lambda ops: (ops[1], ops[2]),
            (backward_in, input_store, used_grad),
        )
        if step_number + 1 < section_count:
            forward_in = lax.ppermute(act_store, "section", [(step_number, step_number + 1)])
            backward_in = lax.ppermute(
                input_store, "section", [(back_section, back_section - 1)]
            )

    grad_scale = 1.0 / math.sqrt(micro_count * tok_rows * shard_count)
    values_t = value_store.reshape(all_rows, value_blocks, tile_width).transpose(1, 2, 0)
    grad_cols = used_grad.reshape(all_rows, model_blocks, tile_width).transpose(1, 0, 2)
    picked = tile_products(out_slot, values_t, grad_cols, model_blocks, 16).astype(jnp.bfloat16)
    received = lax.all_to_all(
        picked.reshape(shard_count, slot_share, tile_width, tile_width), "dp", 0, 0, tiled=True
    )
    summed = received.astype(jnp.float32).sum(axis=0)
    scaled = summed * grad_scale
    out_grad = jnp.where(own_live[:, None, None], scaled, jnp.zeros_like(scaled))
    section_out = act_store.reshape(micro_count, tok_rows, model_width)
    grad_out = input_store.reshape(micro_count, tok_rows, model_width)
    return (section_out[None], grad_out[None], out_grad[None])


def solution(mesh):
    in_specs = (
        P(None, "dp", None),
        P(None, "dp", None),
        P("section", None, None, None),
        P("section", None),
        P("section", "dp", None, None),
        P("section", None),
        P("section", None),
    )
    out_specs = (
        P("section", None, "dp", None),
        P("section", None, "dp", None),
        P("section", "dp", None, None),
    )
    return jax.shard_map(
        on_device, mesh=mesh, in_specs=in_specs, out_specs=out_specs, check_vma=False
    )
```

```python
import math

import jax
import jax.numpy as jnp
from jax import lax
from jax.experimental import pallas as pl
from jax.experimental.pallas import tpu as pltpu
from jax.sharding import PartitionSpec as P

VW = 512
INTERPRET = False
DP_DIMS = (4, 4, 4)
STAGE_AXES = ((1, 0, 2), (0, 1, 2))


def dp_coords(index):
    return [index // (DP_DIMS[1] * DP_DIMS[2]), (index // DP_DIMS[2]) % DP_DIMS[1], index % DP_DIMS[2]]


def dp_index(coords):
    return (coords[0] * DP_DIMS[1] + coords[1]) * DP_DIMS[2] + coords[2]


def shift_pairs(stage, shift, section_count, shard_count):
    pairs = []
    for linear in range(section_count * shard_count):
        section, shard = divmod(linear, shard_count)
        coords = dp_coords(shard)
        axis = STAGE_AXES[section % 2][stage]
        coords[axis] = (coords[axis] + shift) % DP_DIMS[axis]
        pairs.append((linear, section * shard_count + dp_index(coords)))
    return pairs


def ring_reduce(parts, section_count, shard_count):
    for stage in range(3):
        width = DP_DIMS[STAGE_AXES[0][stage]]
        total = parts[0].astype(jnp.float32)
        for shift in range(1, width):
            total = total + lax.ppermute(
                parts[shift], ("section", "dp"), shift_pairs(stage, shift, section_count, shard_count)
            ).astype(jnp.float32)
        parts = total.astype(jnp.bfloat16) if stage < 2 else total
    return parts


def ring_gather(block, section_count, shard_count):
    for stage in reversed(range(3)):
        width = DP_DIMS[STAGE_AXES[0][stage]]
        pieces = [block] + [
            lax.ppermute(
                block, ("section", "dp"), shift_pairs(stage, shift, section_count, shard_count)
            )
            for shift in range(1, width)
        ]
        block = jnp.stack(pieces)
    return block


def slot_maps(section_index, shard_index, out_slot, slot_share):
    odd = section_index % 2 == 1
    mine = dp_coords(shard_index)
    own_axes = [jnp.where(odd, mine[STAGE_AXES[1][n]], mine[STAGE_AXES[0][n]]) for n in range(3)]
    slot_order = jnp.arange(out_slot.shape[0], dtype=jnp.int32)
    owner = dp_coords(slot_order // slot_share)
    owner_axes = [
        jnp.where(odd, owner[STAGE_AXES[1][n]], owner[STAGE_AXES[0][n]]) for n in range(3)
    ]
    behind = [(own_axes[n] - owner_axes[n]) % DP_DIMS[STAGE_AXES[0][n]] for n in range(3)]
    gathered_at = (
        ((behind[0] * DP_DIMS[STAGE_AXES[0][1]] + behind[1]) * DP_DIMS[STAGE_AXES[0][2]] + behind[2])
        * slot_share
        + slot_order % slot_share
    )
    ahead = [
        (own_axes[n] + (slot_order // slot_share) // math.prod(
            DP_DIMS[STAGE_AXES[0][m]] for m in range(n + 1, 3)
        ) % DP_DIMS[STAGE_AXES[0][n]]) % DP_DIMS[STAGE_AXES[0][n]]
        for n in range(3)
    ]
    ahead_yxz = [None, None, None]
    for n in range(3):
        ahead_yxz[STAGE_AXES[0][n]] = ahead[n]
    ahead_odd = [None, None, None]
    for n in range(3):
        ahead_odd[STAGE_AXES[1][n]] = ahead[n]
    send_owner = jnp.where(odd, dp_index(ahead_odd), dp_index(ahead_yxz))
    send_ids = out_slot[send_owner * slot_share + slot_order % slot_share]
    return gathered_at, send_ids


def place_tiles(source, tiles, row_blocks, col_blocks, rows_per_step):
    tile_width = tiles.shape[-1]

    def kernel(source_ref, tiles_ref, out_ref):
        step = pl.program_id(0)
        for row in range(rows_per_step):
            for col in range(col_blocks):
                pick = source_ref[(step * rows_per_step + row) * col_blocks + col]
                tile = tiles_ref[jnp.maximum(pick, 0)]
                tile = jnp.where(pick >= 0, tile, jnp.zeros_like(tile))
                out_ref[
                    row * tile_width : (row + 1) * tile_width,
                    col * tile_width : (col + 1) * tile_width,
                ] = tile

    grid_spec = pltpu.PrefetchScalarGridSpec(
        num_scalar_prefetch=1,
        grid=(row_blocks // rows_per_step,),
        in_specs=[pl.BlockSpec(tiles.shape, lambda step, src: (0, 0, 0))],
        out_specs=pl.BlockSpec(
            (rows_per_step * tile_width, col_blocks * tile_width), lambda step, src: (step, 0)
        ),
    )
    return pl.pallas_call(
        kernel,
        grid_spec=grid_spec,
        out_shape=jax.ShapeDtypeStruct(
            (row_blocks * tile_width, col_blocks * tile_width), tiles.dtype
        ),
        interpret=INTERPRET,
    )(source, tiles)


def tile_products(tile_ids, left_t, right, col_blocks, slots_per_step):
    slot_count = tile_ids.shape[0]
    tile_width = right.shape[-1]

    def kernel(ids_ref, left_ref, right_ref, out_ref):
        step = pl.program_id(0)
        for slot in range(slots_per_step):
            tile = ids_ref[step * slots_per_step + slot]
            out_ref[slot] = jnp.dot(
                left_ref[tile // col_blocks],
                right_ref[tile % col_blocks],
                preferred_element_type=jnp.float32,
            ).astype(out_ref.dtype)

    grid_spec = pltpu.PrefetchScalarGridSpec(
        num_scalar_prefetch=1,
        grid=(slot_count // slots_per_step,),
        in_specs=[
            pl.BlockSpec(left_t.shape, lambda step, ids: (0, 0, 0)),
            pl.BlockSpec(right.shape, lambda step, ids: (0, 0, 0)),
        ],
        out_specs=pl.BlockSpec(
            (slots_per_step, tile_width, tile_width), lambda step, ids: (step, 0, 0)
        ),
    )
    return pl.pallas_call(
        kernel,
        grid_spec=grid_spec,
        out_shape=jax.ShapeDtypeStruct((slot_count, tile_width, tile_width), jnp.bfloat16),
        interpret=INTERPRET,
    )(tile_ids, left_t, right)


def on_device(activations_in, cotangent, value_tiles, value_ids, out_tiles, out_ids, out_count):
    section_index = lax.axis_index("section")
    section_count = lax.axis_size("section")
    shard_count = lax.axis_size("dp")
    shard_index = lax.axis_index("dp")
    micro_count = activations_in.shape[0]
    tok_rows = activations_in.shape[1]
    model_width = activations_in.shape[2]
    all_rows = micro_count * tok_rows
    tile_width = value_tiles.shape[-1]
    value_width = VW
    value_blocks = value_width // tile_width
    model_blocks = model_width // tile_width
    slot_share = out_tiles.shape[1]
    out_slot = out_ids[0]
    live_mask = (jnp.arange(slot_share, dtype=jnp.int32)[None, :] < out_count[0][:, None]).reshape(
        -1
    )
    own_live = lax.dynamic_slice_in_dim(live_mask, shard_index * slot_share, slot_share)
    gathered = ring_gather(out_tiles[0], section_count, shard_count).reshape(
        -1, tile_width, tile_width
    )
    gathered_at, send_ids = slot_maps(section_index, shard_index, out_slot, slot_share)

    tile_numbers = jnp.arange(value_blocks * model_blocks, dtype=jnp.int32)
    value_order = jnp.arange(value_ids.shape[1], dtype=jnp.int32)
    value_source = jnp.max(
        jnp.where(value_ids[0][None, :] == tile_numbers[:, None], value_order[None, :], -1), axis=1
    )
    value_w = place_tiles(value_source, value_tiles[0], model_blocks, value_blocks, 8)
    out_source = jnp.max(
        jnp.where(
            (out_slot[None, :] == tile_numbers[:, None]) & live_mask[None, :],
            gathered_at[None, :],
            -1,
        ),
        axis=1,
    )
    out_w = place_tiles(out_source, gathered, value_blocks, model_blocks, 1)

    def forward_layer(hidden):
        value_rows = jnp.dot(hidden, value_w, preferred_element_type=jnp.float32).astype(
            jnp.bfloat16
        )
        update = jnp.dot(value_rows, out_w, preferred_element_type=jnp.float32)
        result = (hidden.astype(jnp.float32) + update).astype(jnp.bfloat16)
        return value_rows, result

    def backward_layer(grad_rows):
        grad_values = lax.dot_general(
            grad_rows, out_w, (((1,), (1,)), ((), ())), preferred_element_type=jnp.float32
        ).astype(jnp.bfloat16)
        extra_term = lax.dot_general(
            grad_values, value_w, (((1,), (1,)), ((), ())), preferred_element_type=jnp.float32
        )
        return (grad_rows.astype(jnp.float32) + extra_term).astype(jnp.bfloat16)

    first_input = activations_in.reshape(all_rows, model_width)
    last_grad = cotangent.reshape(all_rows, model_width)
    value_store = jnp.zeros((all_rows, value_width), jnp.bfloat16)
    act_store = jnp.zeros((all_rows, model_width), jnp.bfloat16)
    input_store = jnp.zeros((all_rows, model_width), jnp.bfloat16)
    used_grad = jnp.zeros((all_rows, model_width), jnp.bfloat16)
    forward_in = first_input
    backward_in = last_grad
    for step_number in range(section_count):
        back_section = section_count - 1 - step_number
        value_store, act_store = lax.cond(
            section_index == step_number,
            lambda ops: forward_layer(ops[0]),
            lambda ops: (ops[1], ops[2]),
            (forward_in, value_store, act_store),
        )
        input_store, used_grad = lax.cond(
            section_index == back_section,
            lambda ops: (backward_layer(ops[0]), ops[0]),
            lambda ops: (ops[1], ops[2]),
            (backward_in, input_store, used_grad),
        )
        if step_number + 1 < section_count:
            forward_in = lax.ppermute(act_store, "section", [(step_number, step_number + 1)])
            backward_in = lax.ppermute(
                input_store, "section", [(back_section, back_section - 1)]
            )

    grad_scale = 1.0 / math.sqrt(micro_count * tok_rows * shard_count)
    values_t = value_store.reshape(all_rows, value_blocks, tile_width).transpose(1, 2, 0)
    grad_cols = used_grad.reshape(all_rows, model_blocks, tile_width).transpose(1, 0, 2)
    picked = tile_products(send_ids, values_t, grad_cols, model_blocks, 16)
    summed = ring_reduce(
        picked.reshape(*DP_DIMS, slot_share, tile_width, tile_width), section_count, shard_count
    )
    scaled = summed * grad_scale
    out_grad = jnp.where(own_live[:, None, None], scaled, jnp.zeros_like(scaled))
    section_out = act_store.reshape(micro_count, tok_rows, model_width)
    grad_out = input_store.reshape(micro_count, tok_rows, model_width)
    return (section_out[None], grad_out[None], out_grad[None])


def solution(mesh):
    in_specs = (
        P(None, "dp", None),
        P(None, "dp", None),
        P("section", None, None, None),
        P("section", None),
        P("section", "dp", None, None),
        P("section", None),
        P("section", None),
    )
    out_specs = (
        P("section", None, "dp", None),
        P("section", None, "dp", None),
        P("section", "dp", None, None),
    )
    return jax.shard_map(
        on_device, mesh=mesh, in_specs=in_specs, out_specs=out_specs, check_vma=False
    )
```

```python
import math

import jax
import jax.numpy as jnp
from jax import lax
from jax.experimental import pallas as pl
from jax.experimental.pallas import tpu as pltpu
from jax.sharding import PartitionSpec as P

VW = 512
INTERPRET = False
DP_DIMS = (4, 4, 4)
STAGE_AXES = ((1, 0, 2), (0, 1, 2))


def dp_coords(index):
    return [index // (DP_DIMS[1] * DP_DIMS[2]), (index // DP_DIMS[2]) % DP_DIMS[1], index % DP_DIMS[2]]


def dp_index(coords):
    return (coords[0] * DP_DIMS[1] + coords[1]) * DP_DIMS[2] + coords[2]


def shift_pairs(stage, shift, section_count, shard_count):
    pairs = []
    for linear in range(section_count * shard_count):
        section, shard = divmod(linear, shard_count)
        coords = dp_coords(shard)
        axis = STAGE_AXES[section % 2][stage]
        coords[axis] = (coords[axis] + shift) % DP_DIMS[axis]
        pairs.append((linear, section * shard_count + dp_index(coords)))
    return pairs


def ring_reduce(parts, section_count, shard_count):
    for stage in range(3):
        width = DP_DIMS[STAGE_AXES[0][stage]]
        total = parts[0].astype(jnp.float32)
        for shift in range(1, width):
            total = total + lax.ppermute(
                parts[shift], ("section", "dp"), shift_pairs(stage, shift, section_count, shard_count)
            ).astype(jnp.float32)
        parts = total.astype(jnp.bfloat16) if stage < 2 else total
    return parts


def ring_gather(block, section_count, shard_count):
    for stage in reversed(range(3)):
        width = DP_DIMS[STAGE_AXES[0][stage]]
        pieces = [block] + [
            lax.ppermute(
                block, ("section", "dp"), shift_pairs(stage, shift, section_count, shard_count)
            )
            for shift in range(1, width)
        ]
        block = jnp.stack(pieces)
    return block


def slot_maps(section_index, shard_index, out_slot, slot_share):
    odd = section_index % 2 == 1
    mine = dp_coords(shard_index)
    own_axes = [jnp.where(odd, mine[STAGE_AXES[1][n]], mine[STAGE_AXES[0][n]]) for n in range(3)]
    slot_order = jnp.arange(out_slot.shape[0], dtype=jnp.int32)
    owner = dp_coords(slot_order // slot_share)
    owner_axes = [
        jnp.where(odd, owner[STAGE_AXES[1][n]], owner[STAGE_AXES[0][n]]) for n in range(3)
    ]
    behind = [(own_axes[n] - owner_axes[n]) % DP_DIMS[STAGE_AXES[0][n]] for n in range(3)]
    gathered_at = (
        ((behind[0] * DP_DIMS[STAGE_AXES[0][1]] + behind[1]) * DP_DIMS[STAGE_AXES[0][2]] + behind[2])
        * slot_share
        + slot_order % slot_share
    )
    ahead = [
        (own_axes[n] + (slot_order // slot_share) // math.prod(
            DP_DIMS[STAGE_AXES[0][m]] for m in range(n + 1, 3)
        ) % DP_DIMS[STAGE_AXES[0][n]]) % DP_DIMS[STAGE_AXES[0][n]]
        for n in range(3)
    ]
    ahead_yxz = [None, None, None]
    for n in range(3):
        ahead_yxz[STAGE_AXES[0][n]] = ahead[n]
    ahead_odd = [None, None, None]
    for n in range(3):
        ahead_odd[STAGE_AXES[1][n]] = ahead[n]
    send_owner = jnp.where(odd, dp_index(ahead_odd), dp_index(ahead_yxz))
    send_ids = out_slot[send_owner * slot_share + slot_order % slot_share]
    return gathered_at, send_ids


def place_tiles(source, tiles, row_blocks, col_blocks, rows_per_step):
    tile_width = tiles.shape[-1]

    def kernel(source_ref, tiles_ref, out_ref):
        step = pl.program_id(0)
        for row in range(rows_per_step):
            for col in range(col_blocks):
                pick = source_ref[(step * rows_per_step + row) * col_blocks + col]
                tile = tiles_ref[jnp.maximum(pick, 0)]
                tile = jnp.where(pick >= 0, tile, jnp.zeros_like(tile))
                out_ref[
                    row * tile_width : (row + 1) * tile_width,
                    col * tile_width : (col + 1) * tile_width,
                ] = tile

    grid_spec = pltpu.PrefetchScalarGridSpec(
        num_scalar_prefetch=1,
        grid=(row_blocks // rows_per_step,),
        in_specs=[pl.BlockSpec(tiles.shape, lambda step, src: (0, 0, 0))],
        out_specs=pl.BlockSpec(
            (rows_per_step * tile_width, col_blocks * tile_width), lambda step, src: (step, 0)
        ),
    )
    return pl.pallas_call(
        kernel,
        grid_spec=grid_spec,
        out_shape=jax.ShapeDtypeStruct(
            (row_blocks * tile_width, col_blocks * tile_width), tiles.dtype
        ),
        interpret=INTERPRET,
    )(source, tiles)


def tile_products(tile_ids, left_t, right, col_blocks, slots_per_step):
    slot_count = tile_ids.shape[0]
    tile_width = right.shape[-1]

    def kernel(ids_ref, left_ref, right_ref, out_ref):
        step = pl.program_id(0)
        for slot in range(slots_per_step):
            tile = ids_ref[step * slots_per_step + slot]
            out_ref[slot] = jnp.dot(
                left_ref[tile // col_blocks],
                right_ref[tile % col_blocks],
                preferred_element_type=jnp.float32,
            ).astype(out_ref.dtype)

    grid_spec = pltpu.PrefetchScalarGridSpec(
        num_scalar_prefetch=1,
        grid=(slot_count // slots_per_step,),
        in_specs=[
            pl.BlockSpec(left_t.shape, lambda step, ids: (0, 0, 0)),
            pl.BlockSpec(right.shape, lambda step, ids: (0, 0, 0)),
        ],
        out_specs=pl.BlockSpec(
            (slots_per_step, tile_width, tile_width), lambda step, ids: (step, 0, 0)
        ),
    )
    return pl.pallas_call(
        kernel,
        grid_spec=grid_spec,
        out_shape=jax.ShapeDtypeStruct((slot_count, tile_width, tile_width), jnp.bfloat16),
        interpret=INTERPRET,
    )(tile_ids, left_t, right)


def on_device(activations_in, cotangent, value_tiles, value_ids, out_tiles, out_ids, out_count):
    section_index = lax.axis_index("section")
    section_count = lax.axis_size("section")
    shard_count = lax.axis_size("dp")
    shard_index = lax.axis_index("dp")
    micro_count = activations_in.shape[0]
    tok_rows = activations_in.shape[1]
    model_width = activations_in.shape[2]
    all_rows = micro_count * tok_rows
    tile_width = value_tiles.shape[-1]
    value_width = VW
    value_blocks = value_width // tile_width
    model_blocks = model_width // tile_width
    slot_share = out_tiles.shape[1]
    out_slot = out_ids[0]
    live_mask = (jnp.arange(slot_share, dtype=jnp.int32)[None, :] < out_count[0][:, None]).reshape(
        -1
    )
    own_live = lax.dynamic_slice_in_dim(live_mask, shard_index * slot_share, slot_share)
    gathered = ring_gather(out_tiles[0], section_count, shard_count).reshape(
        -1, tile_width, tile_width
    )
    gathered_at, send_ids = slot_maps(section_index, shard_index, out_slot, slot_share)

    tile_numbers = jnp.arange(value_blocks * model_blocks, dtype=jnp.int32)
    value_order = jnp.arange(value_ids.shape[1], dtype=jnp.int32)
    value_source = jnp.max(
        jnp.where(value_ids[0][None, :] == tile_numbers[:, None], value_order[None, :], -1), axis=1
    )
    value_w = place_tiles(value_source, value_tiles[0], model_blocks, value_blocks, 8)
    out_source = (
        jnp.full((value_blocks * model_blocks,), -1, jnp.int32)
        .at[out_slot]
        .set(jnp.where(live_mask, gathered_at, -1), unique_indices=True)
    )
    out_w = place_tiles(out_source, gathered, value_blocks, model_blocks, 1)

    def forward_layer(hidden):
        value_rows = jnp.dot(hidden, value_w, preferred_element_type=jnp.float32).astype(
            jnp.bfloat16
        )
        update = jnp.dot(value_rows, out_w, preferred_element_type=jnp.float32)
        result = (hidden.astype(jnp.float32) + update).astype(jnp.bfloat16)
        return value_rows, result

    def backward_layer(grad_rows):
        grad_values = lax.dot_general(
            grad_rows, out_w, (((1,), (1,)), ((), ())), preferred_element_type=jnp.float32
        ).astype(jnp.bfloat16)
        grad_values = lax.optimization_barrier(grad_values)
        extra_term = lax.dot_general(
            grad_values, value_w, (((1,), (1,)), ((), ())), preferred_element_type=jnp.float32
        )
        return (grad_rows.astype(jnp.float32) + extra_term).astype(jnp.bfloat16)

    first_input = activations_in.reshape(all_rows, model_width)
    last_grad = cotangent.reshape(all_rows, model_width)
    value_store = jnp.zeros((all_rows, value_width), jnp.bfloat16)
    act_store = jnp.zeros((all_rows, model_width), jnp.bfloat16)
    input_store = jnp.zeros((all_rows, model_width), jnp.bfloat16)
    used_grad = jnp.zeros((all_rows, model_width), jnp.bfloat16)
    forward_in = first_input
    backward_in = last_grad
    for step_number in range(section_count):
        back_section = section_count - 1 - step_number
        value_store, act_store = lax.cond(
            section_index == step_number,
            lambda ops: forward_layer(ops[0]),
            lambda ops: (ops[1], ops[2]),
            (forward_in, value_store, act_store),
        )
        input_store, used_grad = lax.cond(
            section_index == back_section,
            lambda ops: (backward_layer(ops[0]), ops[0]),
            lambda ops: (ops[1], ops[2]),
            (backward_in, input_store, used_grad),
        )
        if step_number + 1 < section_count:
            forward_in = lax.ppermute(act_store, "section", [(step_number, step_number + 1)])
            backward_in = lax.ppermute(
                input_store, "section", [(back_section, back_section - 1)]
            )

    grad_scale = 1.0 / math.sqrt(micro_count * tok_rows * shard_count)
    values_t = value_store.reshape(all_rows, value_blocks, tile_width).transpose(1, 2, 0)
    grad_cols = used_grad.reshape(all_rows, model_blocks, tile_width).transpose(1, 0, 2)
    picked = tile_products(send_ids, values_t, grad_cols, model_blocks, 16)
    summed = ring_reduce(
        picked.reshape(*DP_DIMS, slot_share, tile_width, tile_width), section_count, shard_count
    )
    scaled = summed * grad_scale
    out_grad = jnp.where(own_live[:, None, None], scaled, jnp.zeros_like(scaled))
    section_out = act_store.reshape(micro_count, tok_rows, model_width)
    grad_out = input_store.reshape(micro_count, tok_rows, model_width)
    return (section_out[None], grad_out[None], out_grad[None])


def solution(mesh):
    in_specs = (
        P(None, "dp", None),
        P(None, "dp", None),
        P("section", None, None, None),
        P("section", None),
        P("section", "dp", None, None),
        P("section", None),
        P("section", None),
    )
    out_specs = (
        P("section", None, "dp", None),
        P("section", None, "dp", None),
        P("section", "dp", None, None),
    )
    return jax.shard_map(
        on_device, mesh=mesh, in_specs=in_specs, out_specs=out_specs, check_vma=False
    )
```

```python
import math

import jax
import jax.numpy as jnp
from jax import lax
from jax.experimental import pallas as pl
from jax.experimental.pallas import tpu as pltpu
from jax.sharding import PartitionSpec as P

VW = 512
INTERPRET = False
DP_DIMS = (4, 4, 4)
STAGE_AXES = ((1, 0, 2), (0, 1, 2))


def dp_coords(index):
    return [index // (DP_DIMS[1] * DP_DIMS[2]), (index // DP_DIMS[2]) % DP_DIMS[1], index % DP_DIMS[2]]


def dp_index(coords):
    return (coords[0] * DP_DIMS[1] + coords[1]) * DP_DIMS[2] + coords[2]


def shift_pairs(stage, shift, section_count, shard_count):
    pairs = []
    for linear in range(section_count * shard_count):
        section, shard = divmod(linear, shard_count)
        coords = dp_coords(shard)
        axis = STAGE_AXES[section % 2][stage]
        coords[axis] = (coords[axis] + shift) % DP_DIMS[axis]
        pairs.append((linear, section * shard_count + dp_index(coords)))
    return pairs


def ring_reduce(parts, section_count, shard_count):
    for stage in range(3):
        width = DP_DIMS[STAGE_AXES[0][stage]]
        total = parts[0].astype(jnp.float32)
        for shift in range(1, width):
            total = total + lax.ppermute(
                parts[shift], ("section", "dp"), shift_pairs(stage, shift, section_count, shard_count)
            ).astype(jnp.float32)
        parts = total.astype(jnp.bfloat16) if stage < 2 else total
    return parts


def ring_gather(block, section_count, shard_count):
    for stage in reversed(range(3)):
        width = DP_DIMS[STAGE_AXES[0][stage]]
        pieces = [block] + [
            lax.ppermute(
                block, ("section", "dp"), shift_pairs(stage, shift, section_count, shard_count)
            )
            for shift in range(1, width)
        ]
        block = jnp.stack(pieces)
    return block


def slot_maps(section_index, shard_index, out_slot, slot_share):
    odd = section_index % 2 == 1
    mine = dp_coords(shard_index)
    own_axes = [jnp.where(odd, mine[STAGE_AXES[1][n]], mine[STAGE_AXES[0][n]]) for n in range(3)]
    slot_order = jnp.arange(out_slot.shape[0], dtype=jnp.int32)
    owner = dp_coords(slot_order // slot_share)
    owner_axes = [
        jnp.where(odd, owner[STAGE_AXES[1][n]], owner[STAGE_AXES[0][n]]) for n in range(3)
    ]
    behind = [(own_axes[n] - owner_axes[n]) % DP_DIMS[STAGE_AXES[0][n]] for n in range(3)]
    gathered_at = (
        ((behind[0] * DP_DIMS[STAGE_AXES[0][1]] + behind[1]) * DP_DIMS[STAGE_AXES[0][2]] + behind[2])
        * slot_share
        + slot_order % slot_share
    )
    ahead = [
        (own_axes[n] + (slot_order // slot_share) // math.prod(
            DP_DIMS[STAGE_AXES[0][m]] for m in range(n + 1, 3)
        ) % DP_DIMS[STAGE_AXES[0][n]]) % DP_DIMS[STAGE_AXES[0][n]]
        for n in range(3)
    ]
    ahead_yxz = [None, None, None]
    for n in range(3):
        ahead_yxz[STAGE_AXES[0][n]] = ahead[n]
    ahead_odd = [None, None, None]
    for n in range(3):
        ahead_odd[STAGE_AXES[1][n]] = ahead[n]
    send_owner = jnp.where(odd, dp_index(ahead_odd), dp_index(ahead_yxz))
    send_ids = out_slot[send_owner * slot_share + slot_order % slot_share]
    return gathered_at, send_ids


def skinny_matmul(left, right, right_contract, block_k):
    rows, depth = left.shape
    width = right.shape[1 - right_contract]
    steps = depth // block_k
    if right_contract == 0:
        right_spec = pl.BlockSpec((block_k, width), lambda k: (k, 0))
    else:
        right_spec = pl.BlockSpec((width, block_k), lambda k: (0, k))

    def kernel(left_ref, right_ref, out_ref, acc_ref):
        k = pl.program_id(0)

        @pl.when(k == 0)
        def _():
            acc_ref[...] = jnp.zeros_like(acc_ref)

        acc_ref[...] += lax.dot_general(
            left_ref[...],
            right_ref[...],
            (((1,), (right_contract,)), ((), ())),
            preferred_element_type=jnp.float32,
        )

        @pl.when(k == steps - 1)
        def _():
            out_ref[...] = acc_ref[...].astype(out_ref.dtype)

    return pl.pallas_call(
        kernel,
        grid=(steps,),
        in_specs=[pl.BlockSpec((rows, block_k), lambda k: (0, k)), right_spec],
        out_specs=pl.BlockSpec((rows, width), lambda k: (0, 0)),
        out_shape=jax.ShapeDtypeStruct((rows, width), jnp.bfloat16),
        scratch_shapes=[pltpu.VMEM((rows, width), jnp.float32)],
        compiler_params=pltpu.CompilerParams(dimension_semantics=("arbitrary",)),
        interpret=INTERPRET,
    )(left, right)


def place_tiles(source, tiles, row_blocks, col_blocks, rows_per_step):
    tile_width = tiles.shape[-1]

    def kernel(source_ref, tiles_ref, out_ref):
        step = pl.program_id(0)
        for row in range(rows_per_step):
            for col in range(col_blocks):
                pick = source_ref[(step * rows_per_step + row) * col_blocks + col]
                tile = tiles_ref[jnp.maximum(pick, 0)]
                tile = jnp.where(pick >= 0, tile, jnp.zeros_like(tile))
                out_ref[
                    row * tile_width : (row + 1) * tile_width,
                    col * tile_width : (col + 1) * tile_width,
                ] = tile

    grid_spec = pltpu.PrefetchScalarGridSpec(
        num_scalar_prefetch=1,
        grid=(row_blocks // rows_per_step,),
        in_specs=[pl.BlockSpec(tiles.shape, lambda step, src: (0, 0, 0))],
        out_specs=pl.BlockSpec(
            (rows_per_step * tile_width, col_blocks * tile_width), lambda step, src: (step, 0)
        ),
    )
    return pl.pallas_call(
        kernel,
        grid_spec=grid_spec,
        out_shape=jax.ShapeDtypeStruct(
            (row_blocks * tile_width, col_blocks * tile_width), tiles.dtype
        ),
        interpret=INTERPRET,
    )(source, tiles)


def tile_products(tile_ids, left_t, right, col_blocks, slots_per_step):
    slot_count = tile_ids.shape[0]
    tile_width = right.shape[-1]

    def kernel(ids_ref, left_ref, right_ref, out_ref):
        step = pl.program_id(0)
        for slot in range(slots_per_step):
            tile = ids_ref[step * slots_per_step + slot]
            out_ref[slot] = jnp.dot(
                left_ref[tile // col_blocks],
                right_ref[tile % col_blocks],
                preferred_element_type=jnp.float32,
            ).astype(out_ref.dtype)

    grid_spec = pltpu.PrefetchScalarGridSpec(
        num_scalar_prefetch=1,
        grid=(slot_count // slots_per_step,),
        in_specs=[
            pl.BlockSpec(left_t.shape, lambda step, ids: (0, 0, 0)),
            pl.BlockSpec(right.shape, lambda step, ids: (0, 0, 0)),
        ],
        out_specs=pl.BlockSpec(
            (slots_per_step, tile_width, tile_width), lambda step, ids: (step, 0, 0)
        ),
    )
    return pl.pallas_call(
        kernel,
        grid_spec=grid_spec,
        out_shape=jax.ShapeDtypeStruct((slot_count, tile_width, tile_width), jnp.bfloat16),
        interpret=INTERPRET,
    )(tile_ids, left_t, right)


def on_device(activations_in, cotangent, value_tiles, value_ids, out_tiles, out_ids, out_count):
    section_index = lax.axis_index("section")
    section_count = lax.axis_size("section")
    shard_count = lax.axis_size("dp")
    shard_index = lax.axis_index("dp")
    micro_count = activations_in.shape[0]
    tok_rows = activations_in.shape[1]
    model_width = activations_in.shape[2]
    all_rows = micro_count * tok_rows
    tile_width = value_tiles.shape[-1]
    value_width = VW
    value_blocks = value_width // tile_width
    model_blocks = model_width // tile_width
    slot_share = out_tiles.shape[1]
    out_slot = out_ids[0]
    live_mask = (jnp.arange(slot_share, dtype=jnp.int32)[None, :] < out_count[0][:, None]).reshape(
        -1
    )
    own_live = lax.dynamic_slice_in_dim(live_mask, shard_index * slot_share, slot_share)
    gathered = ring_gather(out_tiles[0], section_count, shard_count).reshape(
        -1, tile_width, tile_width
    )
    gathered_at, send_ids = slot_maps(section_index, shard_index, out_slot, slot_share)

    tile_numbers = jnp.arange(value_blocks * model_blocks, dtype=jnp.int32)
    value_order = jnp.arange(value_ids.shape[1], dtype=jnp.int32)
    value_source = jnp.max(
        jnp.where(value_ids[0][None, :] == tile_numbers[:, None], value_order[None, :], -1), axis=1
    )
    value_w = place_tiles(value_source, value_tiles[0], model_blocks, value_blocks, 8)
    out_source = (
        jnp.full((value_blocks * model_blocks,), -1, jnp.int32)
        .at[out_slot]
        .set(jnp.where(live_mask, gathered_at, -1), unique_indices=True)
    )
    out_w = place_tiles(out_source, gathered, value_blocks, model_blocks, 1)

    def forward_layer(hidden):
        value_rows = skinny_matmul(hidden, value_w, 0, 2048)
        update = jnp.dot(value_rows, out_w, preferred_element_type=jnp.float32)
        result = (hidden.astype(jnp.float32) + update).astype(jnp.bfloat16)
        return value_rows, result

    def backward_layer(grad_rows):
        grad_values = skinny_matmul(grad_rows, out_w, 1, 2048)
        extra_term = lax.dot_general(
            grad_values, value_w, (((1,), (1,)), ((), ())), preferred_element_type=jnp.float32
        )
        return (grad_rows.astype(jnp.float32) + extra_term).astype(jnp.bfloat16)

    first_input = activations_in.reshape(all_rows, model_width)
    last_grad = cotangent.reshape(all_rows, model_width)
    value_store = jnp.zeros((all_rows, value_width), jnp.bfloat16)
    act_store = jnp.zeros((all_rows, model_width), jnp.bfloat16)
    input_store = jnp.zeros((all_rows, model_width), jnp.bfloat16)
    used_grad = jnp.zeros((all_rows, model_width), jnp.bfloat16)
    forward_in = first_input
    backward_in = last_grad
    for step_number in range(section_count):
        back_section = section_count - 1 - step_number
        value_store, act_store = lax.cond(
            section_index == step_number,
            lambda ops: forward_layer(ops[0]),
            lambda ops: (ops[1], ops[2]),
            (forward_in, value_store, act_store),
        )
        input_store, used_grad = lax.cond(
            section_index == back_section,
            lambda ops: (backward_layer(ops[0]), ops[0]),
            lambda ops: (ops[1], ops[2]),
            (backward_in, input_store, used_grad),
        )
        if step_number + 1 < section_count:
            forward_in = lax.ppermute(act_store, "section", [(step_number, step_number + 1)])
            backward_in = lax.ppermute(
                input_store, "section", [(back_section, back_section - 1)]
            )

    grad_scale = 1.0 / math.sqrt(micro_count * tok_rows * shard_count)
    values_t = value_store.reshape(all_rows, value_blocks, tile_width).transpose(1, 2, 0)
    grad_cols = used_grad.reshape(all_rows, model_blocks, tile_width).transpose(1, 0, 2)
    picked = tile_products(send_ids, values_t, grad_cols, model_blocks, 16)
    summed = ring_reduce(
        picked.reshape(*DP_DIMS, slot_share, tile_width, tile_width), section_count, shard_count
    )
    scaled = summed * grad_scale
    out_grad = jnp.where(own_live[:, None, None], scaled, jnp.zeros_like(scaled))
    section_out = act_store.reshape(micro_count, tok_rows, model_width)
    grad_out = input_store.reshape(micro_count, tok_rows, model_width)
    return (section_out[None], grad_out[None], out_grad[None])


def solution(mesh):
    in_specs = (
        P(None, "dp", None),
        P(None, "dp", None),
        P("section", None, None, None),
        P("section", None),
        P("section", "dp", None, None),
        P("section", None),
        P("section", None),
    )
    out_specs = (
        P("section", None, "dp", None),
        P("section", None, "dp", None),
        P("section", "dp", None, None),
    )
    return jax.shard_map(
        on_device, mesh=mesh, in_specs=in_specs, out_specs=out_specs, check_vma=False
    )
```

```python
import math

import jax
import jax.numpy as jnp
from jax import lax
from jax.experimental import pallas as pl
from jax.experimental.pallas import tpu as pltpu
from jax.sharding import PartitionSpec as P

VW = 512
INTERPRET = False
DP_DIMS = (4, 4, 4)
STAGE_AXES = ((1, 0, 2), (0, 1, 2))


def dp_coords(index):
    return [index // (DP_DIMS[1] * DP_DIMS[2]), (index // DP_DIMS[2]) % DP_DIMS[1], index % DP_DIMS[2]]


def dp_index(coords):
    return (coords[0] * DP_DIMS[1] + coords[1]) * DP_DIMS[2] + coords[2]


def shift_pairs(stage, shift, section_count, shard_count):
    pairs = []
    for linear in range(section_count * shard_count):
        section, shard = divmod(linear, shard_count)
        coords = dp_coords(shard)
        axis = STAGE_AXES[section % 2][stage]
        coords[axis] = (coords[axis] + shift) % DP_DIMS[axis]
        pairs.append((linear, section * shard_count + dp_index(coords)))
    return pairs


def ring_reduce(parts, section_count, shard_count):
    for stage in range(3):
        width = DP_DIMS[STAGE_AXES[0][stage]]
        total = parts[0].astype(jnp.float32)
        for shift in range(1, width):
            total = total + lax.ppermute(
                parts[shift], ("section", "dp"), shift_pairs(stage, shift, section_count, shard_count)
            ).astype(jnp.float32)
        parts = total.astype(jnp.bfloat16) if stage < 2 else total
    return parts


def ring_gather(block, section_count, shard_count):
    for stage in reversed(range(3)):
        width = DP_DIMS[STAGE_AXES[0][stage]]
        pieces = [block] + [
            lax.ppermute(
                block, ("section", "dp"), shift_pairs(stage, shift, section_count, shard_count)
            )
            for shift in range(1, width)
        ]
        block = jnp.stack(pieces)
    return block


def slot_maps(section_index, shard_index, out_slot, slot_share):
    odd = section_index % 2 == 1
    mine = dp_coords(shard_index)
    own_axes = [jnp.where(odd, mine[STAGE_AXES[1][n]], mine[STAGE_AXES[0][n]]) for n in range(3)]
    slot_order = jnp.arange(out_slot.shape[0], dtype=jnp.int32)
    owner = dp_coords(slot_order // slot_share)
    owner_axes = [
        jnp.where(odd, owner[STAGE_AXES[1][n]], owner[STAGE_AXES[0][n]]) for n in range(3)
    ]
    behind = [(own_axes[n] - owner_axes[n]) % DP_DIMS[STAGE_AXES[0][n]] for n in range(3)]
    gathered_at = (
        ((behind[0] * DP_DIMS[STAGE_AXES[0][1]] + behind[1]) * DP_DIMS[STAGE_AXES[0][2]] + behind[2])
        * slot_share
        + slot_order % slot_share
    )
    ahead = [
        (own_axes[n] + (slot_order // slot_share) // math.prod(
            DP_DIMS[STAGE_AXES[0][m]] for m in range(n + 1, 3)
        ) % DP_DIMS[STAGE_AXES[0][n]]) % DP_DIMS[STAGE_AXES[0][n]]
        for n in range(3)
    ]
    ahead_yxz = [None, None, None]
    for n in range(3):
        ahead_yxz[STAGE_AXES[0][n]] = ahead[n]
    ahead_odd = [None, None, None]
    for n in range(3):
        ahead_odd[STAGE_AXES[1][n]] = ahead[n]
    send_owner = jnp.where(odd, dp_index(ahead_odd), dp_index(ahead_yxz))
    send_ids = out_slot[send_owner * slot_share + slot_order % slot_share]
    return gathered_at, send_ids


def place_tiles(source, tiles, row_blocks, col_blocks, rows_per_step):
    tile_width = tiles.shape[-1]

    def kernel(source_ref, tiles_ref, out_ref):
        step = pl.program_id(0)
        for row in range(rows_per_step):
            for col in range(col_blocks):
                pick = source_ref[(step * rows_per_step + row) * col_blocks + col]
                tile = tiles_ref[jnp.maximum(pick, 0)]
                tile = jnp.where(pick >= 0, tile, jnp.zeros_like(tile))
                out_ref[
                    row * tile_width : (row + 1) * tile_width,
                    col * tile_width : (col + 1) * tile_width,
                ] = tile

    grid_spec = pltpu.PrefetchScalarGridSpec(
        num_scalar_prefetch=1,
        grid=(row_blocks // rows_per_step,),
        in_specs=[pl.BlockSpec(tiles.shape, lambda step, src: (0, 0, 0))],
        out_specs=pl.BlockSpec(
            (rows_per_step * tile_width, col_blocks * tile_width), lambda step, src: (step, 0)
        ),
    )
    return pl.pallas_call(
        kernel,
        grid_spec=grid_spec,
        out_shape=jax.ShapeDtypeStruct(
            (row_blocks * tile_width, col_blocks * tile_width), tiles.dtype
        ),
        interpret=INTERPRET,
    )(source, tiles)


def tile_products(tile_ids, left_t, right, col_blocks, slots_per_step):
    slot_count = tile_ids.shape[0]
    tile_width = left_t.shape[-2]

    def kernel(ids_ref, left_ref, right_ref, out_ref):
        step = pl.program_id(0)
        for slot in range(slots_per_step):
            tile = ids_ref[step * slots_per_step + slot]
            start = pl.multiple_of((tile % col_blocks) * tile_width, tile_width)
            out_ref[slot] = jnp.dot(
                left_ref[tile // col_blocks],
                right_ref[:, pl.ds(start, tile_width)],
                preferred_element_type=jnp.float32,
            ).astype(out_ref.dtype)

    grid_spec = pltpu.PrefetchScalarGridSpec(
        num_scalar_prefetch=1,
        grid=(slot_count // slots_per_step,),
        in_specs=[
            pl.BlockSpec(left_t.shape, lambda step, ids: (0, 0, 0)),
            pl.BlockSpec(right.shape, lambda step, ids: (0, 0)),
        ],
        out_specs=pl.BlockSpec(
            (slots_per_step, tile_width, tile_width), lambda step, ids: (step, 0, 0)
        ),
    )
    return pl.pallas_call(
        kernel,
        grid_spec=grid_spec,
        out_shape=jax.ShapeDtypeStruct((slot_count, tile_width, tile_width), jnp.bfloat16),
        interpret=INTERPRET,
    )(tile_ids, left_t, right)


def on_device(activations_in, cotangent, value_tiles, value_ids, out_tiles, out_ids, out_count):
    section_index = lax.axis_index("section")
    section_count = lax.axis_size("section")
    shard_count = lax.axis_size("dp")
    shard_index = lax.axis_index("dp")
    micro_count = activations_in.shape[0]
    tok_rows = activations_in.shape[1]
    model_width = activations_in.shape[2]
    all_rows = micro_count * tok_rows
    tile_width = value_tiles.shape[-1]
    value_width = VW
    value_blocks = value_width // tile_width
    model_blocks = model_width // tile_width
    slot_share = out_tiles.shape[1]
    out_slot = out_ids[0]
    live_mask = (jnp.arange(slot_share, dtype=jnp.int32)[None, :] < out_count[0][:, None]).reshape(
        -1
    )
    own_live = lax.dynamic_slice_in_dim(live_mask, shard_index * slot_share, slot_share)
    gathered = ring_gather(out_tiles[0], section_count, shard_count).reshape(
        -1, tile_width, tile_width
    )
    gathered_at, send_ids = slot_maps(section_index, shard_index, out_slot, slot_share)

    tile_numbers = jnp.arange(value_blocks * model_blocks, dtype=jnp.int32)
    value_order = jnp.arange(value_ids.shape[1], dtype=jnp.int32)
    value_source = jnp.max(
        jnp.where(value_ids[0][None, :] == tile_numbers[:, None], value_order[None, :], -1), axis=1
    )
    value_w = place_tiles(value_source, value_tiles[0], model_blocks, value_blocks, 8)
    out_source = (
        jnp.full((value_blocks * model_blocks,), -1, jnp.int32)
        .at[out_slot]
        .set(jnp.where(live_mask, gathered_at, -1), unique_indices=True)
    )
    out_w = place_tiles(out_source, gathered, value_blocks, model_blocks, 1)

    def forward_layer(hidden):
        value_rows = jnp.dot(hidden, value_w, preferred_element_type=jnp.float32).astype(
            jnp.bfloat16
        )
        update = jnp.dot(value_rows, out_w, preferred_element_type=jnp.float32)
        result = (hidden.astype(jnp.float32) + update).astype(jnp.bfloat16)
        return value_rows, result

    def backward_layer(grad_rows):
        grad_values = lax.dot_general(
            grad_rows, out_w, (((1,), (1,)), ((), ())), preferred_element_type=jnp.float32
        ).astype(jnp.bfloat16)
        grad_values = lax.optimization_barrier(grad_values)
        extra_term = lax.dot_general(
            grad_values, value_w, (((1,), (1,)), ((), ())), preferred_element_type=jnp.float32
        )
        return (grad_rows.astype(jnp.float32) + extra_term).astype(jnp.bfloat16)

    first_input = activations_in.reshape(all_rows, model_width)
    last_grad = cotangent.reshape(all_rows, model_width)
    value_store = jnp.zeros((all_rows, value_width), jnp.bfloat16)
    act_store = jnp.zeros((all_rows, model_width), jnp.bfloat16)
    input_store = jnp.zeros((all_rows, model_width), jnp.bfloat16)
    used_grad = jnp.zeros((all_rows, model_width), jnp.bfloat16)
    forward_in = first_input
    backward_in = last_grad
    for step_number in range(section_count):
        back_section = section_count - 1 - step_number
        value_store, act_store = lax.cond(
            section_index == step_number,
            lambda ops: forward_layer(ops[0]),
            lambda ops: (ops[1], ops[2]),
            (forward_in, value_store, act_store),
        )
        input_store, used_grad = lax.cond(
            section_index == back_section,
            lambda ops: (backward_layer(ops[0]), ops[0]),
            lambda ops: (ops[1], ops[2]),
            (backward_in, input_store, used_grad),
        )
        if step_number + 1 < section_count:
            outgoing = jnp.where(section_index == step_number, act_store, input_store)
            incoming = lax.ppermute(
                outgoing,
                "section",
                [(step_number, step_number + 1), (back_section, back_section - 1)],
            )
            forward_in = incoming
            backward_in = incoming

    grad_scale = 1.0 / math.sqrt(micro_count * tok_rows * shard_count)
    values_t = value_store.reshape(all_rows, value_blocks, tile_width).transpose(1, 2, 0)
    picked = tile_products(send_ids, values_t, used_grad, model_blocks, 16)
    summed = ring_reduce(
        picked.reshape(*DP_DIMS, slot_share, tile_width, tile_width), section_count, shard_count
    )
    scaled = summed * grad_scale
    out_grad = jnp.where(own_live[:, None, None], scaled, jnp.zeros_like(scaled))
    section_out = act_store.reshape(micro_count, tok_rows, model_width)
    grad_out = input_store.reshape(micro_count, tok_rows, model_width)
    return (section_out[None], grad_out[None], out_grad[None])


def solution(mesh):
    in_specs = (
        P(None, "dp", None),
        P(None, "dp", None),
        P("section", None, None, None),
        P("section", None),
        P("section", "dp", None, None),
        P("section", None),
        P("section", None),
    )
    out_specs = (
        P("section", None, "dp", None),
        P("section", None, "dp", None),
        P("section", "dp", None, None),
    )
    return jax.shard_map(
        on_device, mesh=mesh, in_specs=in_specs, out_specs=out_specs, check_vma=False
    )
```

```python
import math

import jax
import jax.numpy as jnp
from jax import lax
from jax.experimental import pallas as pl
from jax.experimental.pallas import tpu as pltpu
from jax.sharding import PartitionSpec as P

VW = 512
INTERPRET = False
DP_DIMS = (4, 4, 4)
STAGE_AXES = ((1, 0, 2), (0, 1, 2))


def dp_coords(index):
    return [index // (DP_DIMS[1] * DP_DIMS[2]), (index // DP_DIMS[2]) % DP_DIMS[1], index % DP_DIMS[2]]


def dp_index(coords):
    return (coords[0] * DP_DIMS[1] + coords[1]) * DP_DIMS[2] + coords[2]


def shift_pairs(stage, shift, section_count, shard_count):
    pairs = []
    for linear in range(section_count * shard_count):
        section, shard = divmod(linear, shard_count)
        coords = dp_coords(shard)
        axis = STAGE_AXES[section % 2][stage]
        coords[axis] = (coords[axis] + shift) % DP_DIMS[axis]
        pairs.append((linear, section * shard_count + dp_index(coords)))
    return pairs


def ring_reduce(parts, section_count, shard_count):
    for stage in range(3):
        width = DP_DIMS[STAGE_AXES[0][stage]]
        total = parts[0].astype(jnp.float32)
        for shift in range(1, width):
            total = total + lax.ppermute(
                parts[shift], ("section", "dp"), shift_pairs(stage, shift, section_count, shard_count)
            ).astype(jnp.float32)
        parts = total.astype(jnp.bfloat16) if stage < 2 else total
    return parts


def ring_gather(block, section_count, shard_count):
    for stage in reversed(range(3)):
        width = DP_DIMS[STAGE_AXES[0][stage]]
        pieces = [block] + [
            lax.ppermute(
                block, ("section", "dp"), shift_pairs(stage, shift, section_count, shard_count)
            )
            for shift in range(1, width)
        ]
        if stage == 0:
            return pieces
        block = jnp.stack(pieces)


def slot_maps(section_index, shard_index, out_slot, slot_share):
    odd = section_index % 2 == 1
    mine = dp_coords(shard_index)
    own_axes = [jnp.where(odd, mine[STAGE_AXES[1][n]], mine[STAGE_AXES[0][n]]) for n in range(3)]
    slot_order = jnp.arange(out_slot.shape[0], dtype=jnp.int32)
    owner = dp_coords(slot_order // slot_share)
    owner_axes = [
        jnp.where(odd, owner[STAGE_AXES[1][n]], owner[STAGE_AXES[0][n]]) for n in range(3)
    ]
    behind = [(own_axes[n] - owner_axes[n]) % DP_DIMS[STAGE_AXES[0][n]] for n in range(3)]
    gathered_at = (
        ((behind[0] * DP_DIMS[STAGE_AXES[0][1]] + behind[1]) * DP_DIMS[STAGE_AXES[0][2]] + behind[2])
        * slot_share
        + slot_order % slot_share
    )
    ahead = [
        (own_axes[n] + (slot_order // slot_share) // math.prod(
            DP_DIMS[STAGE_AXES[0][m]] for m in range(n + 1, 3)
        ) % DP_DIMS[STAGE_AXES[0][n]]) % DP_DIMS[STAGE_AXES[0][n]]
        for n in range(3)
    ]
    ahead_yxz = [None, None, None]
    for n in range(3):
        ahead_yxz[STAGE_AXES[0][n]] = ahead[n]
    ahead_odd = [None, None, None]
    for n in range(3):
        ahead_odd[STAGE_AXES[1][n]] = ahead[n]
    send_owner = jnp.where(odd, dp_index(ahead_odd), dp_index(ahead_yxz))
    send_ids = out_slot[send_owner * slot_share + slot_order % slot_share]
    return gathered_at, send_ids


def place_tiles(source, tile_sets, row_blocks, col_blocks, rows_per_step):
    tile_width = tile_sets[0].shape[-1]
    set_size = tile_sets[0].shape[0]

    def kernel(source_ref, *refs):
        tiles_refs, out_ref = refs[:-1], refs[-1]
        step = pl.program_id(0)
        for row in range(rows_per_step):
            for col in range(col_blocks):
                pick = source_ref[(step * rows_per_step + row) * col_blocks + col]
                rows = slice(row * tile_width, (row + 1) * tile_width)
                cols = slice(col * tile_width, (col + 1) * tile_width)

                @pl.when(pick < 0)
                def _():
                    out_ref[rows, cols] = jnp.zeros((tile_width, tile_width), out_ref.dtype)

                for number, tiles_ref in enumerate(tiles_refs):

                    @pl.when((pick >= number * set_size) & (pick < (number + 1) * set_size))
                    def _():
                        out_ref[rows, cols] = tiles_ref[pick - number * set_size]

    grid_spec = pltpu.PrefetchScalarGridSpec(
        num_scalar_prefetch=1,
        grid=(row_blocks // rows_per_step,),
        in_specs=[pl.BlockSpec(tiles.shape, lambda step, src: (0, 0, 0)) for tiles in tile_sets],
        out_specs=pl.BlockSpec(
            (rows_per_step * tile_width, col_blocks * tile_width), lambda step, src: (step, 0)
        ),
    )
    return pl.pallas_call(
        kernel,
        grid_spec=grid_spec,
        out_shape=jax.ShapeDtypeStruct(
            (row_blocks * tile_width, col_blocks * tile_width), tile_sets[0].dtype
        ),
        interpret=INTERPRET,
    )(source, *tile_sets)


def tile_products(tile_ids, left_t, right, col_blocks, slots_per_step):
    slot_count = tile_ids.shape[0]
    tile_width = left_t.shape[-2]

    def kernel(ids_ref, left_ref, right_ref, out_ref):
        step = pl.program_id(0)
        for slot in range(slots_per_step):
            tile = ids_ref[step * slots_per_step + slot]
            start = pl.multiple_of((tile % col_blocks) * tile_width, tile_width)
            out_ref[slot] = jnp.dot(
                left_ref[tile // col_blocks],
                right_ref[:, pl.ds(start, tile_width)],
                preferred_element_type=jnp.float32,
            ).astype(out_ref.dtype)

    grid_spec = pltpu.PrefetchScalarGridSpec(
        num_scalar_prefetch=1,
        grid=(slot_count // slots_per_step,),
        in_specs=[
            pl.BlockSpec(left_t.shape, lambda step, ids: (0, 0, 0)),
            pl.BlockSpec(right.shape, lambda step, ids: (0, 0)),
        ],
        out_specs=pl.BlockSpec(
            (slots_per_step, tile_width, tile_width), lambda step, ids: (step, 0, 0)
        ),
    )
    return pl.pallas_call(
        kernel,
        grid_spec=grid_spec,
        out_shape=jax.ShapeDtypeStruct((slot_count, tile_width, tile_width), jnp.bfloat16),
        interpret=INTERPRET,
    )(tile_ids, left_t, right)


def on_device(activations_in, cotangent, value_tiles, value_ids, out_tiles, out_ids, out_count):
    section_index = lax.axis_index("section")
    section_count = lax.axis_size("section")
    shard_count = lax.axis_size("dp")
    shard_index = lax.axis_index("dp")
    micro_count = activations_in.shape[0]
    tok_rows = activations_in.shape[1]
    model_width = activations_in.shape[2]
    all_rows = micro_count * tok_rows
    tile_width = value_tiles.shape[-1]
    value_width = VW
    value_blocks = value_width // tile_width
    model_blocks = model_width // tile_width
    slot_share = out_tiles.shape[1]
    out_slot = out_ids[0]
    live_mask = (jnp.arange(slot_share, dtype=jnp.int32)[None, :] < out_count[0][:, None]).reshape(
        -1
    )
    own_live = lax.dynamic_slice_in_dim(live_mask, shard_index * slot_share, slot_share)
    gathered = [
        piece.reshape(-1, tile_width, tile_width)
        for piece in ring_gather(out_tiles[0], section_count, shard_count)
    ]
    gathered_at, send_ids = slot_maps(section_index, shard_index, out_slot, slot_share)

    tile_numbers = jnp.arange(value_blocks * model_blocks, dtype=jnp.int32)
    value_order = jnp.arange(value_ids.shape[1], dtype=jnp.int32)
    value_source = jnp.max(
        jnp.where(value_ids[0][None, :] == tile_numbers[:, None], value_order[None, :], -1), axis=1
    )
    value_w = place_tiles(value_source, [value_tiles[0]], model_blocks, value_blocks, 8)
    out_source = (
        jnp.full((value_blocks * model_blocks,), -1, jnp.int32)
        .at[out_slot]
        .set(jnp.where(live_mask, gathered_at, -1), unique_indices=True)
    )
    out_w = place_tiles(out_source, gathered, value_blocks, model_blocks, 1)

    def forward_layer(hidden):
        value_rows = jnp.dot(hidden, value_w, preferred_element_type=jnp.float32).astype(
            jnp.bfloat16
        )
        update = jnp.dot(value_rows, out_w, preferred_element_type=jnp.float32)
        result = (hidden.astype(jnp.float32) + update).astype(jnp.bfloat16)
        return value_rows, result

    def backward_layer(grad_rows):
        grad_values = lax.dot_general(
            grad_rows, out_w, (((1,), (1,)), ((), ())), preferred_element_type=jnp.float32
        ).astype(jnp.bfloat16)
        grad_values = lax.optimization_barrier(grad_values)
        extra_term = lax.dot_general(
            grad_values, value_w, (((1,), (1,)), ((), ())), preferred_element_type=jnp.float32
        )
        return (grad_rows.astype(jnp.float32) + extra_term).astype(jnp.bfloat16)

    first_input = activations_in.reshape(all_rows, model_width)
    last_grad = cotangent.reshape(all_rows, model_width)
    value_store = jnp.zeros((all_rows, value_width), jnp.bfloat16)
    act_store = jnp.zeros((all_rows, model_width), jnp.bfloat16)
    input_store = jnp.zeros((all_rows, model_width), jnp.bfloat16)
    used_grad = jnp.zeros((all_rows, model_width), jnp.bfloat16)
    forward_in = first_input
    backward_in = last_grad
    for step_number in range(section_count):
        back_section = section_count - 1 - step_number
        value_store, act_store = lax.cond(
            section_index == step_number,
            lambda ops: forward_layer(ops[0]),
            lambda ops: (ops[1], ops[2]),
            (forward_in, value_store, act_store),
        )
        input_store, used_grad = lax.cond(
            section_index == back_section,
            lambda ops: (backward_layer(ops[0]), ops[0]),
            lambda ops: (ops[1], ops[2]),
            (backward_in, input_store, used_grad),
        )
        if step_number + 1 < section_count:
            outgoing = jnp.where(section_index == step_number, act_store, input_store)
            incoming = lax.ppermute(
                outgoing,
                "section",
                [(step_number, step_number + 1), (back_section, back_section - 1)],
            )
            forward_in = incoming
            backward_in = incoming

    grad_scale = 1.0 / math.sqrt(micro_count * tok_rows * shard_count)
    values_t = value_store.reshape(all_rows, value_blocks, tile_width).transpose(1, 2, 0)
    picked = tile_products(send_ids, values_t, used_grad, model_blocks, 16)
    summed = ring_reduce(
        picked.reshape(*DP_DIMS, slot_share, tile_width, tile_width), section_count, shard_count
    )
    scaled = summed * grad_scale
    out_grad = jnp.where(own_live[:, None, None], scaled, jnp.zeros_like(scaled))
    section_out = act_store.reshape(micro_count, tok_rows, model_width)
    grad_out = input_store.reshape(micro_count, tok_rows, model_width)
    return (section_out[None], grad_out[None], out_grad[None])


def solution(mesh):
    in_specs = (
        P(None, "dp", None),
        P(None, "dp", None),
        P("section", None, None, None),
        P("section", None),
        P("section", "dp", None, None),
        P("section", None),
        P("section", None),
    )
    out_specs = (
        P("section", None, "dp", None),
        P("section", None, "dp", None),
        P("section", "dp", None, None),
    )
    return jax.shard_map(
        on_device, mesh=mesh, in_specs=in_specs, out_specs=out_specs, check_vma=False
    )
```

```python
import math

import jax
import jax.numpy as jnp
from jax import lax
from jax.experimental import pallas as pl
from jax.experimental.pallas import tpu as pltpu
from jax.sharding import PartitionSpec as P

VW = 512
INTERPRET = False
DP_DIMS = (4, 4, 4)
STAGE_AXES = ((1, 0, 2), (0, 1, 2))


def dp_coords(index):
    return [index // (DP_DIMS[1] * DP_DIMS[2]), (index // DP_DIMS[2]) % DP_DIMS[1], index % DP_DIMS[2]]


def dp_index(coords):
    return (coords[0] * DP_DIMS[1] + coords[1]) * DP_DIMS[2] + coords[2]


def shift_pairs(stage, shift, section_count, shard_count):
    pairs = []
    for linear in range(section_count * shard_count):
        section, shard = divmod(linear, shard_count)
        coords = dp_coords(shard)
        axis = STAGE_AXES[section % 2][stage]
        coords[axis] = (coords[axis] + shift) % DP_DIMS[axis]
        pairs.append((linear, section * shard_count + dp_index(coords)))
    return pairs


def ring_reduce(parts, section_count, shard_count):
    for stage in range(3):
        width = DP_DIMS[STAGE_AXES[0][stage]]
        total = parts[0].astype(jnp.float32)
        for shift in range(1, width):
            total = total + lax.ppermute(
                parts[shift], ("section", "dp"), shift_pairs(stage, shift, section_count, shard_count)
            ).astype(jnp.float32)
        parts = total.astype(jnp.bfloat16) if stage < 2 else total
    return parts


def ring_gather(block, section_count, shard_count):
    for stage in reversed(range(3)):
        width = DP_DIMS[STAGE_AXES[0][stage]]
        pieces = [block] + [
            lax.ppermute(
                block, ("section", "dp"), shift_pairs(stage, shift, section_count, shard_count)
            )
            for shift in range(1, width)
        ]
        block = jnp.stack(pieces)
    return block


def slot_maps(section_index, shard_index, out_slot, slot_share):
    odd = section_index % 2 == 1
    mine = dp_coords(shard_index)
    own_axes = [jnp.where(odd, mine[STAGE_AXES[1][n]], mine[STAGE_AXES[0][n]]) for n in range(3)]
    slot_order = jnp.arange(out_slot.shape[0], dtype=jnp.int32)
    owner = dp_coords(slot_order // slot_share)
    owner_axes = [
        jnp.where(odd, owner[STAGE_AXES[1][n]], owner[STAGE_AXES[0][n]]) for n in range(3)
    ]
    behind = [(own_axes[n] - owner_axes[n]) % DP_DIMS[STAGE_AXES[0][n]] for n in range(3)]
    gathered_at = (
        ((behind[0] * DP_DIMS[STAGE_AXES[0][1]] + behind[1]) * DP_DIMS[STAGE_AXES[0][2]] + behind[2])
        * slot_share
        + slot_order % slot_share
    )
    ahead = [
        (own_axes[n] + (slot_order // slot_share) // math.prod(
            DP_DIMS[STAGE_AXES[0][m]] for m in range(n + 1, 3)
        ) % DP_DIMS[STAGE_AXES[0][n]]) % DP_DIMS[STAGE_AXES[0][n]]
        for n in range(3)
    ]
    ahead_yxz = [None, None, None]
    for n in range(3):
        ahead_yxz[STAGE_AXES[0][n]] = ahead[n]
    ahead_odd = [None, None, None]
    for n in range(3):
        ahead_odd[STAGE_AXES[1][n]] = ahead[n]
    send_owner = jnp.where(odd, dp_index(ahead_odd), dp_index(ahead_yxz))
    send_ids = out_slot[send_owner * slot_share + slot_order % slot_share]
    return gathered_at, send_ids


def place_tiles(source, tiles, row_blocks, col_blocks, rows_per_step):
    tile_width = tiles.shape[-1]

    def kernel(source_ref, tiles_ref, out_ref):
        step = pl.program_id(0)
        for row in range(rows_per_step):
            for col in range(col_blocks):
                pick = source_ref[(step * rows_per_step + row) * col_blocks + col]
                tile = tiles_ref[jnp.maximum(pick, 0)]
                tile = jnp.where(pick >= 0, tile, jnp.zeros_like(tile))
                out_ref[
                    row * tile_width : (row + 1) * tile_width,
                    col * tile_width : (col + 1) * tile_width,
                ] = tile

    grid_spec = pltpu.PrefetchScalarGridSpec(
        num_scalar_prefetch=1,
        grid=(row_blocks // rows_per_step,),
        in_specs=[pl.BlockSpec(tiles.shape, lambda step, src: (0, 0, 0))],
        out_specs=pl.BlockSpec(
            (rows_per_step * tile_width, col_blocks * tile_width), lambda step, src: (step, 0)
        ),
    )
    return pl.pallas_call(
        kernel,
        grid_spec=grid_spec,
        out_shape=jax.ShapeDtypeStruct(
            (row_blocks * tile_width, col_blocks * tile_width), tiles.dtype
        ),
        interpret=INTERPRET,
    )(source, tiles)


def tile_products(tile_ids, left_t, right, col_blocks, slots_per_step):
    slot_count = tile_ids.shape[0]
    tile_width = left_t.shape[-2]

    def kernel(ids_ref, left_ref, right_ref, out_ref):
        step = pl.program_id(0)
        for slot in range(slots_per_step):
            tile = ids_ref[step * slots_per_step + slot]
            start = pl.multiple_of((tile % col_blocks) * tile_width, tile_width)
            out_ref[slot] = jnp.dot(
                left_ref[tile // col_blocks],
                right_ref[:, pl.ds(start, tile_width)],
                preferred_element_type=jnp.float32,
            ).astype(out_ref.dtype)

    grid_spec = pltpu.PrefetchScalarGridSpec(
        num_scalar_prefetch=1,
        grid=(slot_count // slots_per_step,),
        in_specs=[
            pl.BlockSpec(left_t.shape, lambda step, ids: (0, 0, 0)),
            pl.BlockSpec(right.shape, lambda step, ids: (0, 0)),
        ],
        out_specs=pl.BlockSpec(
            (slots_per_step, tile_width, tile_width), lambda step, ids: (step, 0, 0)
        ),
    )
    return pl.pallas_call(
        kernel,
        grid_spec=grid_spec,
        out_shape=jax.ShapeDtypeStruct((slot_count, tile_width, tile_width), jnp.bfloat16),
        interpret=INTERPRET,
    )(tile_ids, left_t, right)


def on_device(activations_in, cotangent, value_tiles, value_ids, out_tiles, out_ids, out_count):
    section_index = lax.axis_index("section")
    section_count = lax.axis_size("section")
    shard_count = lax.axis_size("dp")
    shard_index = lax.axis_index("dp")
    micro_count = activations_in.shape[0]
    tok_rows = activations_in.shape[1]
    model_width = activations_in.shape[2]
    all_rows = micro_count * tok_rows
    tile_width = value_tiles.shape[-1]
    value_width = VW
    value_blocks = value_width // tile_width
    model_blocks = model_width // tile_width
    slot_share = out_tiles.shape[1]
    out_slot = out_ids[0]
    live_mask = (jnp.arange(slot_share, dtype=jnp.int32)[None, :] < out_count[0][:, None]).reshape(
        -1
    )
    own_live = lax.dynamic_slice_in_dim(live_mask, shard_index * slot_share, slot_share)
    gathered = ring_gather(out_tiles[0], section_count, shard_count).reshape(
        -1, tile_width, tile_width
    )
    gathered_at, send_ids = slot_maps(section_index, shard_index, out_slot, slot_share)

    tile_numbers = jnp.arange(value_blocks * model_blocks, dtype=jnp.int32)
    value_order = jnp.arange(value_ids.shape[1], dtype=jnp.int32)
    value_source = jnp.max(
        jnp.where(value_ids[0][None, :] == tile_numbers[:, None], value_order[None, :], -1), axis=1
    )
    value_w = place_tiles(value_source, value_tiles[0], model_blocks, value_blocks, 8)
    out_source = (
        jnp.full((value_blocks * model_blocks,), -1, jnp.int32)
        .at[out_slot]
        .set(jnp.where(live_mask, gathered_at, -1), unique_indices=True)
    )
    out_w = place_tiles(out_source, gathered, value_blocks, model_blocks, 1)

    def forward_layer(hidden):
        value_rows = jnp.dot(hidden, value_w, preferred_element_type=jnp.float32).astype(
            jnp.bfloat16
        )
        update = jnp.dot(value_rows, out_w, preferred_element_type=jnp.float32)
        result = (hidden.astype(jnp.float32) + update).astype(jnp.bfloat16)
        return value_rows, result

    def backward_layer(grad_rows):
        grad_values = lax.dot_general(
            grad_rows, out_w, (((1,), (1,)), ((), ())), preferred_element_type=jnp.float32
        ).astype(jnp.bfloat16)
        grad_values = lax.optimization_barrier(grad_values)
        extra_term = lax.dot_general(
            grad_values, value_w, (((1,), (1,)), ((), ())), preferred_element_type=jnp.float32
        )
        return (grad_rows.astype(jnp.float32) + extra_term).astype(jnp.bfloat16)

    first_input = activations_in.reshape(all_rows, model_width)
    last_grad = cotangent.reshape(all_rows, model_width)
    value_store = jnp.zeros((all_rows, value_width), jnp.bfloat16)
    act_store = jnp.zeros((all_rows, model_width), jnp.bfloat16)
    input_store = jnp.zeros((all_rows, model_width), jnp.bfloat16)
    used_grad = jnp.zeros((all_rows, model_width), jnp.bfloat16)
    forward_in = first_input
    backward_in = last_grad
    for step_number in range(section_count):
        back_section = section_count - 1 - step_number
        value_store, act_store = lax.cond(
            section_index == step_number,
            lambda ops: forward_layer(ops[0]),
            lambda ops: (ops[1], ops[2]),
            (forward_in, value_store, act_store),
        )
        input_store, used_grad = lax.cond(
            section_index == back_section,
            lambda ops: (backward_layer(ops[0]), ops[0]),
            lambda ops: (ops[1], ops[2]),
            (backward_in, input_store, used_grad),
        )
        if step_number + 1 < section_count:
            outgoing = jnp.where(section_index == step_number, act_store, input_store)
            incoming = lax.ppermute(
                outgoing,
                "section",
                [(step_number, step_number + 1), (back_section, back_section - 1)],
            )
            forward_in = incoming
            backward_in = incoming

    grad_scale = 1.0 / math.sqrt(micro_count * tok_rows * shard_count)
    values_t = value_store.reshape(all_rows, value_blocks, tile_width).transpose(1, 2, 0)
    block_slots = send_ids.shape[0] // DP_DIMS[STAGE_AXES[0][0]]
    picked = [
        tile_products(
            send_ids[number * block_slots : (number + 1) * block_slots],
            values_t,
            used_grad,
            model_blocks,
            16,
        ).reshape(*DP_DIMS[1:], slot_share, tile_width, tile_width)
        for number in range(DP_DIMS[STAGE_AXES[0][0]])
    ]
    summed = ring_reduce(picked, section_count, shard_count)
    scaled = summed * grad_scale
    out_grad = jnp.where(own_live[:, None, None], scaled, jnp.zeros_like(scaled))
    section_out = act_store.reshape(micro_count, tok_rows, model_width)
    grad_out = input_store.reshape(micro_count, tok_rows, model_width)
    return (section_out[None], grad_out[None], out_grad[None])


def solution(mesh):
    in_specs = (
        P(None, "dp", None),
        P(None, "dp", None),
        P("section", None, None, None),
        P("section", None),
        P("section", "dp", None, None),
        P("section", None),
        P("section", None),
    )
    out_specs = (
        P("section", None, "dp", None),
        P("section", None, "dp", None),
        P("section", "dp", None, None),
    )
    return jax.shard_map(
        on_device, mesh=mesh, in_specs=in_specs, out_specs=out_specs, check_vma=False
    )
```

```python
import math

import jax
import jax.numpy as jnp
from jax import lax
from jax.experimental import pallas as pl
from jax.experimental.pallas import tpu as pltpu
from jax.sharding import PartitionSpec as P

VW = 512
INTERPRET = False
DP_DIMS = (4, 4, 4)
STAGE_AXES = ((1, 0, 2), (0, 1, 2))


def dp_coords(index):
    return [index // (DP_DIMS[1] * DP_DIMS[2]), (index // DP_DIMS[2]) % DP_DIMS[1], index % DP_DIMS[2]]


def dp_index(coords):
    return (coords[0] * DP_DIMS[1] + coords[1]) * DP_DIMS[2] + coords[2]


def shift_pairs(stage, shift, section_count, shard_count):
    pairs = []
    for linear in range(section_count * shard_count):
        section, shard = divmod(linear, shard_count)
        coords = dp_coords(shard)
        axis = STAGE_AXES[section % 2][stage]
        coords[axis] = (coords[axis] + shift) % DP_DIMS[axis]
        pairs.append((linear, section * shard_count + dp_index(coords)))
    return pairs


def ring_reduce(parts, section_count, shard_count):
    for stage in range(3):
        width = DP_DIMS[STAGE_AXES[0][stage]]
        total = parts[0].astype(jnp.float32)
        for shift in range(1, width):
            if stage == 0 and shift == 2:
                half = parts[shift].shape[0] // 2
                straight = lax.ppermute(
                    parts[shift][:half], ("section", "dp"),
                    shift_pairs(stage, shift, section_count, shard_count),
                )
                relayed = parts[shift][half:]
                for _ in range(2):
                    relayed = lax.ppermute(
                        relayed, ("section", "dp"), shift_pairs(stage, -1, section_count, shard_count)
                    )
                total = total + jnp.concatenate([straight, relayed]).astype(jnp.float32)
                continue
            total = total + lax.ppermute(
                parts[shift], ("section", "dp"), shift_pairs(stage, shift, section_count, shard_count)
            ).astype(jnp.float32)
        parts = total.astype(jnp.bfloat16) if stage < 2 else total
    return parts


def ring_gather(block, section_count, shard_count):
    for stage in reversed(range(3)):
        width = DP_DIMS[STAGE_AXES[0][stage]]
        pieces = [block]
        for shift in range(1, width):
            if stage == 0 and shift == 2:
                half = block.shape[0] // 2
                straight = lax.ppermute(
                    block[:half], ("section", "dp"),
                    shift_pairs(stage, shift, section_count, shard_count),
                )
                relayed = block[half:]
                for _ in range(2):
                    relayed = lax.ppermute(
                        relayed, ("section", "dp"), shift_pairs(stage, 1, section_count, shard_count)
                    )
                pieces.append(jnp.concatenate([straight, relayed]))
                continue
            pieces.append(
                lax.ppermute(
                    block, ("section", "dp"), shift_pairs(stage, shift, section_count, shard_count)
                )
            )
        block = jnp.stack(pieces)
    return block


def slot_maps(section_index, shard_index, out_slot, slot_share):
    odd = section_index % 2 == 1
    mine = dp_coords(shard_index)
    own_axes = [jnp.where(odd, mine[STAGE_AXES[1][n]], mine[STAGE_AXES[0][n]]) for n in range(3)]
    slot_order = jnp.arange(out_slot.shape[0], dtype=jnp.int32)
    owner = dp_coords(slot_order // slot_share)
    owner_axes = [
        jnp.where(odd, owner[STAGE_AXES[1][n]], owner[STAGE_AXES[0][n]]) for n in range(3)
    ]
    behind = [(own_axes[n] - owner_axes[n]) % DP_DIMS[STAGE_AXES[0][n]] for n in range(3)]
    gathered_at = (
        ((behind[0] * DP_DIMS[STAGE_AXES[0][1]] + behind[1]) * DP_DIMS[STAGE_AXES[0][2]] + behind[2])
        * slot_share
        + slot_order % slot_share
    )
    ahead = [
        (own_axes[n] + (slot_order // slot_share) // math.prod(
            DP_DIMS[STAGE_AXES[0][m]] for m in range(n + 1, 3)
        ) % DP_DIMS[STAGE_AXES[0][n]]) % DP_DIMS[STAGE_AXES[0][n]]
        for n in range(3)
    ]
    ahead_yxz = [None, None, None]
    for n in range(3):
        ahead_yxz[STAGE_AXES[0][n]] = ahead[n]
    ahead_odd = [None, None, None]
    for n in range(3):
        ahead_odd[STAGE_AXES[1][n]] = ahead[n]
    send_owner = jnp.where(odd, dp_index(ahead_odd), dp_index(ahead_yxz))
    send_ids = out_slot[send_owner * slot_share + slot_order % slot_share]
    return gathered_at, send_ids


def place_tiles(source, tiles, row_blocks, col_blocks, rows_per_step):
    tile_width = tiles.shape[-1]

    def kernel(source_ref, tiles_ref, out_ref):
        step = pl.program_id(0)
        for row in range(rows_per_step):
            for col in range(col_blocks):
                pick = source_ref[(step * rows_per_step + row) * col_blocks + col]
                tile = tiles_ref[jnp.maximum(pick, 0)]
                tile = jnp.where(pick >= 0, tile, jnp.zeros_like(tile))
                out_ref[
                    row * tile_width : (row + 1) * tile_width,
                    col * tile_width : (col + 1) * tile_width,
                ] = tile

    grid_spec = pltpu.PrefetchScalarGridSpec(
        num_scalar_prefetch=1,
        grid=(row_blocks // rows_per_step,),
        in_specs=[pl.BlockSpec(tiles.shape, lambda step, src: (0, 0, 0))],
        out_specs=pl.BlockSpec(
            (rows_per_step * tile_width, col_blocks * tile_width), lambda step, src: (step, 0)
        ),
    )
    return pl.pallas_call(
        kernel,
        grid_spec=grid_spec,
        out_shape=jax.ShapeDtypeStruct(
            (row_blocks * tile_width, col_blocks * tile_width), tiles.dtype
        ),
        interpret=INTERPRET,
    )(source, tiles)


def tile_products(tile_ids, left_t, right, col_blocks, slots_per_step):
    slot_count = tile_ids.shape[0]
    tile_width = left_t.shape[-2]

    def kernel(ids_ref, left_ref, right_ref, out_ref):
        step = pl.program_id(0)
        for slot in range(slots_per_step):
            tile = ids_ref[step * slots_per_step + slot]
            start = pl.multiple_of((tile % col_blocks) * tile_width, tile_width)
            out_ref[slot] = jnp.dot(
                left_ref[tile // col_blocks],
                right_ref[:, pl.ds(start, tile_width)],
                preferred_element_type=jnp.float32,
            ).astype(out_ref.dtype)

    grid_spec = pltpu.PrefetchScalarGridSpec(
        num_scalar_prefetch=1,
        grid=(slot_count // slots_per_step,),
        in_specs=[
            pl.BlockSpec(left_t.shape, lambda step, ids: (0, 0, 0)),
            pl.BlockSpec(right.shape, lambda step, ids: (0, 0)),
        ],
        out_specs=pl.BlockSpec(
            (slots_per_step, tile_width, tile_width), lambda step, ids: (step, 0, 0)
        ),
    )
    return pl.pallas_call(
        kernel,
        grid_spec=grid_spec,
        out_shape=jax.ShapeDtypeStruct((slot_count, tile_width, tile_width), jnp.bfloat16),
        interpret=INTERPRET,
    )(tile_ids, left_t, right)


def on_device(activations_in, cotangent, value_tiles, value_ids, out_tiles, out_ids, out_count):
    section_index = lax.axis_index("section")
    section_count = lax.axis_size("section")
    shard_count = lax.axis_size("dp")
    shard_index = lax.axis_index("dp")
    micro_count = activations_in.shape[0]
    tok_rows = activations_in.shape[1]
    model_width = activations_in.shape[2]
    all_rows = micro_count * tok_rows
    tile_width = value_tiles.shape[-1]
    value_width = VW
    value_blocks = value_width // tile_width
    model_blocks = model_width // tile_width
    slot_share = out_tiles.shape[1]
    out_slot = out_ids[0]
    live_mask = (jnp.arange(slot_share, dtype=jnp.int32)[None, :] < out_count[0][:, None]).reshape(
        -1
    )
    own_live = lax.dynamic_slice_in_dim(live_mask, shard_index * slot_share, slot_share)
    gathered = ring_gather(out_tiles[0], section_count, shard_count).reshape(
        -1, tile_width, tile_width
    )
    gathered_at, send_ids = slot_maps(section_index, shard_index, out_slot, slot_share)

    tile_numbers = jnp.arange(value_blocks * model_blocks, dtype=jnp.int32)
    value_order = jnp.arange(value_ids.shape[1], dtype=jnp.int32)
    value_source = jnp.max(
        jnp.where(value_ids[0][None, :] == tile_numbers[:, None], value_order[None, :], -1), axis=1
    )
    value_w = place_tiles(value_source, value_tiles[0], model_blocks, value_blocks, 8)
    out_source = (
        jnp.full((value_blocks * model_blocks,), -1, jnp.int32)
        .at[out_slot]
        .set(jnp.where(live_mask, gathered_at, -1), unique_indices=True)
    )
    out_w = place_tiles(out_source, gathered, value_blocks, model_blocks, 1)

    def forward_layer(hidden):
        value_rows = jnp.dot(hidden, value_w, preferred_element_type=jnp.float32).astype(
            jnp.bfloat16
        )
        update = jnp.dot(value_rows, out_w, preferred_element_type=jnp.float32)
        result = (hidden.astype(jnp.float32) + update).astype(jnp.bfloat16)
        return value_rows, result

    def backward_layer(grad_rows):
        grad_values = lax.dot_general(
            grad_rows, out_w, (((1,), (1,)), ((), ())), preferred_element_type=jnp.float32
        ).astype(jnp.bfloat16)
        grad_values = lax.optimization_barrier(grad_values)
        extra_term = lax.dot_general(
            grad_values, value_w, (((1,), (1,)), ((), ())), preferred_element_type=jnp.float32
        )
        return (grad_rows.astype(jnp.float32) + extra_term).astype(jnp.bfloat16)

    first_input = activations_in.reshape(all_rows, model_width)
    last_grad = cotangent.reshape(all_rows, model_width)
    value_store = jnp.zeros((all_rows, value_width), jnp.bfloat16)
    act_store = jnp.zeros((all_rows, model_width), jnp.bfloat16)
    input_store = jnp.zeros((all_rows, model_width), jnp.bfloat16)
    used_grad = jnp.zeros((all_rows, model_width), jnp.bfloat16)
    forward_in = first_input
    backward_in = last_grad
    for step_number in range(section_count):
        back_section = section_count - 1 - step_number
        value_store, act_store = lax.cond(
            section_index == step_number,
            lambda ops: forward_layer(ops[0]),
            lambda ops: (ops[1], ops[2]),
            (forward_in, value_store, act_store),
        )
        input_store, used_grad = lax.cond(
            section_index == back_section,
            lambda ops: (backward_layer(ops[0]), ops[0]),
            lambda ops: (ops[1], ops[2]),
            (backward_in, input_store, used_grad),
        )
        if step_number + 1 < section_count:
            outgoing = jnp.where(section_index == step_number, act_store, input_store)
            incoming = lax.ppermute(
                outgoing,
                "section",
                [(step_number, step_number + 1), (back_section, back_section - 1)],
            )
            forward_in = incoming
            backward_in = incoming

    grad_scale = 1.0 / math.sqrt(micro_count * tok_rows * shard_count)
    values_t = value_store.reshape(all_rows, value_blocks, tile_width).transpose(1, 2, 0)
    picked = tile_products(send_ids, values_t, used_grad, model_blocks, 16)
    summed = ring_reduce(
        picked.reshape(*DP_DIMS, slot_share, tile_width, tile_width), section_count, shard_count
    )
    scaled = summed * grad_scale
    out_grad = jnp.where(own_live[:, None, None], scaled, jnp.zeros_like(scaled))
    section_out = act_store.reshape(micro_count, tok_rows, model_width)
    grad_out = input_store.reshape(micro_count, tok_rows, model_width)
    return (section_out[None], grad_out[None], out_grad[None])


def solution(mesh):
    in_specs = (
        P(None, "dp", None),
        P(None, "dp", None),
        P("section", None, None, None),
        P("section", None),
        P("section", "dp", None, None),
        P("section", None),
        P("section", None),
    )
    out_specs = (
        P("section", None, "dp", None),
        P("section", None, "dp", None),
        P("section", "dp", None, None),
    )
    return jax.shard_map(
        on_device, mesh=mesh, in_specs=in_specs, out_specs=out_specs, check_vma=False
    )
```

```python
import math

import jax
import jax.numpy as jnp
from jax import lax
from jax.experimental import pallas as pl
from jax.experimental.pallas import tpu as pltpu
from jax.sharding import PartitionSpec as P

VW = 512
INTERPRET = False
DP_DIMS = (4, 4, 4)
STAGE_AXES = ((1, 0, 2), (0, 1, 2))


def dp_coords(index):
    return [index // (DP_DIMS[1] * DP_DIMS[2]), (index // DP_DIMS[2]) % DP_DIMS[1], index % DP_DIMS[2]]


def dp_index(coords):
    return (coords[0] * DP_DIMS[1] + coords[1]) * DP_DIMS[2] + coords[2]


def shift_pairs(stage, shift, section_count, shard_count):
    pairs = []
    for linear in range(section_count * shard_count):
        section, shard = divmod(linear, shard_count)
        coords = dp_coords(shard)
        axis = STAGE_AXES[section % 2][stage]
        coords[axis] = (coords[axis] + shift) % DP_DIMS[axis]
        pairs.append((linear, section * shard_count + dp_index(coords)))
    return pairs


def ring_reduce(parts, section_count, shard_count):
    for stage in range(3):
        width = DP_DIMS[STAGE_AXES[0][stage]]
        total = parts[0].astype(jnp.float32)
        for shift in range(1, width):
            total = total + lax.ppermute(
                parts[shift], ("section", "dp"), shift_pairs(stage, shift, section_count, shard_count)
            ).astype(jnp.float32)
        parts = total.astype(jnp.bfloat16) if stage < 2 else total
    return parts


def ring_gather(block, section_count, shard_count):
    for stage in reversed(range(3)):
        width = DP_DIMS[STAGE_AXES[0][stage]]
        pieces = [block] + [
            lax.ppermute(
                block, ("section", "dp"), shift_pairs(stage, shift, section_count, shard_count)
            )
            for shift in range(1, width)
        ]
        block = jnp.stack(pieces)
    return block


def slot_maps(section_index, shard_index, out_slot, slot_share):
    odd = section_index % 2 == 1
    mine = dp_coords(shard_index)
    own_axes = [jnp.where(odd, mine[STAGE_AXES[1][n]], mine[STAGE_AXES[0][n]]) for n in range(3)]
    slot_order = jnp.arange(out_slot.shape[0], dtype=jnp.int32)
    owner = dp_coords(slot_order // slot_share)
    owner_axes = [
        jnp.where(odd, owner[STAGE_AXES[1][n]], owner[STAGE_AXES[0][n]]) for n in range(3)
    ]
    behind = [(own_axes[n] - owner_axes[n]) % DP_DIMS[STAGE_AXES[0][n]] for n in range(3)]
    gathered_at = (
        ((behind[0] * DP_DIMS[STAGE_AXES[0][1]] + behind[1]) * DP_DIMS[STAGE_AXES[0][2]] + behind[2])
        * slot_share
        + slot_order % slot_share
    )
    ahead = [
        (own_axes[n] + (slot_order // slot_share) // math.prod(
            DP_DIMS[STAGE_AXES[0][m]] for m in range(n + 1, 3)
        ) % DP_DIMS[STAGE_AXES[0][n]]) % DP_DIMS[STAGE_AXES[0][n]]
        for n in range(3)
    ]
    ahead_yxz = [None, None, None]
    for n in range(3):
        ahead_yxz[STAGE_AXES[0][n]] = ahead[n]
    ahead_odd = [None, None, None]
    for n in range(3):
        ahead_odd[STAGE_AXES[1][n]] = ahead[n]
    send_owner = jnp.where(odd, dp_index(ahead_odd), dp_index(ahead_yxz))
    send_ids = out_slot[send_owner * slot_share + slot_order % slot_share]
    return gathered_at, send_ids


def place_tiles(source, tiles, row_blocks, col_blocks, rows_per_step):
    tile_width = tiles.shape[-1]

    def kernel(source_ref, tiles_ref, out_ref):
        step = pl.program_id(0)
        for row in range(rows_per_step):
            for col in range(col_blocks):
                pick = source_ref[(step * rows_per_step + row) * col_blocks + col]
                tile = tiles_ref[jnp.maximum(pick, 0)]
                tile = jnp.where(pick >= 0, tile, jnp.zeros_like(tile))
                out_ref[
                    row * tile_width : (row + 1) * tile_width,
                    col * tile_width : (col + 1) * tile_width,
                ] = tile

    grid_spec = pltpu.PrefetchScalarGridSpec(
        num_scalar_prefetch=1,
        grid=(row_blocks // rows_per_step,),
        in_specs=[pl.BlockSpec(tiles.shape, lambda step, src: (0, 0, 0))],
        out_specs=pl.BlockSpec(
            (rows_per_step * tile_width, col_blocks * tile_width), lambda step, src: (step, 0)
        ),
    )
    return pl.pallas_call(
        kernel,
        grid_spec=grid_spec,
        out_shape=jax.ShapeDtypeStruct(
            (row_blocks * tile_width, col_blocks * tile_width), tiles.dtype
        ),
        interpret=INTERPRET,
    )(source, tiles)


def tile_products(tile_ids, left_t, right, col_blocks, slots_per_step):
    slot_count = tile_ids.shape[0]
    tile_width = left_t.shape[-2]

    def kernel(ids_ref, left_ref, right_ref, out_ref):
        step = pl.program_id(0)
        for slot in range(slots_per_step):
            tile = ids_ref[step * slots_per_step + slot]
            start = pl.multiple_of((tile % col_blocks) * tile_width, tile_width)
            out_ref[slot] = jnp.dot(
                left_ref[tile // col_blocks],
                right_ref[:, pl.ds(start, tile_width)],
                preferred_element_type=jnp.float32,
            ).astype(out_ref.dtype)

    grid_spec = pltpu.PrefetchScalarGridSpec(
        num_scalar_prefetch=1,
        grid=(slot_count // slots_per_step,),
        in_specs=[
            pl.BlockSpec(left_t.shape, lambda step, ids: (0, 0, 0)),
            pl.BlockSpec(right.shape, lambda step, ids: (0, 0)),
        ],
        out_specs=pl.BlockSpec(
            (slots_per_step, tile_width, tile_width), lambda step, ids: (step, 0, 0)
        ),
    )
    return pl.pallas_call(
        kernel,
        grid_spec=grid_spec,
        out_shape=jax.ShapeDtypeStruct((slot_count, tile_width, tile_width), jnp.bfloat16),
        interpret=INTERPRET,
    )(tile_ids, left_t, right)


def on_device(activations_in, cotangent, value_tiles, value_ids, out_tiles, out_ids, out_count):
    section_index = lax.axis_index("section")
    section_count = lax.axis_size("section")
    shard_count = lax.axis_size("dp")
    shard_index = lax.axis_index("dp")
    micro_count = activations_in.shape[0]
    tok_rows = activations_in.shape[1]
    model_width = activations_in.shape[2]
    all_rows = micro_count * tok_rows
    tile_width = value_tiles.shape[-1]
    value_width = VW
    value_blocks = value_width // tile_width
    model_blocks = model_width // tile_width
    slot_share = out_tiles.shape[1]
    out_slot = out_ids[0]
    live_mask = (jnp.arange(slot_share, dtype=jnp.int32)[None, :] < out_count[0][:, None]).reshape(
        -1
    )
    own_live = lax.dynamic_slice_in_dim(live_mask, shard_index * slot_share, slot_share)
    gathered = ring_gather(out_tiles[0], section_count, shard_count).reshape(
        -1, tile_width, tile_width
    )
    gathered_at, send_ids = slot_maps(section_index, shard_index, out_slot, slot_share)

    tile_numbers = jnp.arange(value_blocks * model_blocks, dtype=jnp.int32)
    value_order = jnp.arange(value_ids.shape[1], dtype=jnp.int32)
    value_source = jnp.max(
        jnp.where(value_ids[0][None, :] == tile_numbers[:, None], value_order[None, :], -1), axis=1
    )
    value_w = place_tiles(value_source, value_tiles[0], model_blocks, value_blocks, 8)
    out_source = (
        jnp.full((value_blocks * model_blocks,), -1, jnp.int32)
        .at[out_slot]
        .set(jnp.where(live_mask, gathered_at, -1), unique_indices=True)
    )
    out_w = place_tiles(out_source, gathered, value_blocks, model_blocks, 1)

    def forward_layer(hidden):
        value_rows = jnp.dot(hidden, value_w, preferred_element_type=jnp.float32).astype(
            jnp.bfloat16
        )
        update = jnp.dot(value_rows, out_w, preferred_element_type=jnp.float32)
        result = (hidden.astype(jnp.float32) + update).astype(jnp.bfloat16)
        return value_rows, result

    def backward_layer(grad_rows):
        grad_values = lax.dot_general(
            grad_rows, out_w, (((1,), (1,)), ((), ())), preferred_element_type=jnp.float32
        ).astype(jnp.bfloat16)
        grad_values = lax.optimization_barrier(grad_values)
        extra_term = lax.dot_general(
            grad_values, value_w, (((1,), (1,)), ((), ())), preferred_element_type=jnp.float32
        )
        return (grad_rows.astype(jnp.float32) + extra_term).astype(jnp.bfloat16)

    first_input = activations_in.reshape(all_rows, model_width)
    last_grad = cotangent.reshape(all_rows, model_width)
    value_store = jnp.zeros((all_rows, value_width), jnp.bfloat16)
    act_store = jnp.zeros((all_rows, model_width), jnp.bfloat16)
    input_store = jnp.zeros((all_rows, model_width), jnp.bfloat16)
    used_grad = jnp.zeros((all_rows, model_width), jnp.bfloat16)
    forward_in = first_input
    backward_in = last_grad
    for step_number in range(section_count):
        back_section = section_count - 1 - step_number
        value_store, act_store = lax.cond(
            section_index == step_number,
            lambda ops: forward_layer(ops[0]),
            lambda ops: (ops[1], ops[2]),
            (forward_in, value_store, act_store),
        )
        input_store, used_grad = lax.cond(
            section_index == back_section,
            lambda ops: (backward_layer(ops[0]), ops[0]),
            lambda ops: (ops[1], ops[2]),
            (backward_in, input_store, used_grad),
        )
        if step_number + 1 < section_count:
            outgoing = jnp.where(section_index == step_number, act_store, input_store)
            incoming = lax.ppermute(
                outgoing,
                "section",
                [(step_number, step_number + 1), (back_section, back_section - 1)],
            )
            forward_in = incoming
            backward_in = incoming

    grad_scale = 1.0 / math.sqrt(micro_count * tok_rows * shard_count)
    values_t = value_store.reshape(all_rows, value_blocks, tile_width).transpose(1, 2, 0)
    picked = tile_products(send_ids, values_t, used_grad, model_blocks, 48)
    summed = ring_reduce(
        picked.reshape(*DP_DIMS, slot_share, tile_width, tile_width), section_count, shard_count
    )
    scaled = summed * grad_scale
    out_grad = jnp.where(own_live[:, None, None], scaled, jnp.zeros_like(scaled))
    section_out = act_store.reshape(micro_count, tok_rows, model_width)
    grad_out = input_store.reshape(micro_count, tok_rows, model_width)
    return (section_out[None], grad_out[None], out_grad[None])


def solution(mesh):
    in_specs = (
        P(None, "dp", None),
        P(None, "dp", None),
        P("section", None, None, None),
        P("section", None),
        P("section", "dp", None, None),
        P("section", None),
        P("section", None),
    )
    out_specs = (
        P("section", None, "dp", None),
        P("section", None, "dp", None),
        P("section", "dp", None, None),
    )
    return jax.shard_map(
        on_device, mesh=mesh, in_specs=in_specs, out_specs=out_specs, check_vma=False
    )
```

```python
import math

import jax
import jax.numpy as jnp
from jax import lax
from jax.experimental import pallas as pl
from jax.experimental.pallas import tpu as pltpu
from jax.sharding import PartitionSpec as P

VW = 512
INTERPRET = False
DP_DIMS = (4, 4, 4)
STAGE_AXES = ((1, 0, 2), (0, 1, 2))


def dp_coords(index):
    return [index // (DP_DIMS[1] * DP_DIMS[2]), (index // DP_DIMS[2]) % DP_DIMS[1], index % DP_DIMS[2]]


def dp_index(coords):
    return (coords[0] * DP_DIMS[1] + coords[1]) * DP_DIMS[2] + coords[2]


def shift_pairs(stage, shift, section_count, shard_count):
    pairs = []
    for linear in range(section_count * shard_count):
        section, shard = divmod(linear, shard_count)
        coords = dp_coords(shard)
        axis = STAGE_AXES[section % 2][stage]
        coords[axis] = (coords[axis] + shift) % DP_DIMS[axis]
        pairs.append((linear, section * shard_count + dp_index(coords)))
    return pairs


def ring_reduce(parts, section_count, shard_count):
    for stage in range(3):
        width = DP_DIMS[STAGE_AXES[0][stage]]
        total = parts[0].astype(jnp.float32)
        for shift in range(1, width):
            total = total + lax.ppermute(
                parts[shift], ("section", "dp"), shift_pairs(stage, shift, section_count, shard_count)
            ).astype(jnp.float32)
        parts = total.astype(jnp.bfloat16) if stage < 2 else total
    return parts


def ring_gather(block, section_count, shard_count):
    for stage in reversed(range(3)):
        width = DP_DIMS[STAGE_AXES[0][stage]]
        pieces = [block] + [
            lax.ppermute(
                block, ("section", "dp"), shift_pairs(stage, shift, section_count, shard_count)
            )
            for shift in range(1, width)
        ]
        block = jnp.stack(pieces)
    return block


def slot_maps(section_index, shard_index, out_slot, slot_share):
    odd = section_index % 2 == 1
    mine = dp_coords(shard_index)
    own_axes = [jnp.where(odd, mine[STAGE_AXES[1][n]], mine[STAGE_AXES[0][n]]) for n in range(3)]
    slot_order = jnp.arange(out_slot.shape[0], dtype=jnp.int32)
    owner = dp_coords(slot_order // slot_share)
    owner_axes = [
        jnp.where(odd, owner[STAGE_AXES[1][n]], owner[STAGE_AXES[0][n]]) for n in range(3)
    ]
    behind = [(own_axes[n] - owner_axes[n]) % DP_DIMS[STAGE_AXES[0][n]] for n in range(3)]
    gathered_at = (
        ((behind[0] * DP_DIMS[STAGE_AXES[0][1]] + behind[1]) * DP_DIMS[STAGE_AXES[0][2]] + behind[2])
        * slot_share
        + slot_order % slot_share
    )
    ahead = [
        (own_axes[n] + (slot_order // slot_share) // math.prod(
            DP_DIMS[STAGE_AXES[0][m]] for m in range(n + 1, 3)
        ) % DP_DIMS[STAGE_AXES[0][n]]) % DP_DIMS[STAGE_AXES[0][n]]
        for n in range(3)
    ]
    ahead_yxz = [None, None, None]
    for n in range(3):
        ahead_yxz[STAGE_AXES[0][n]] = ahead[n]
    ahead_odd = [None, None, None]
    for n in range(3):
        ahead_odd[STAGE_AXES[1][n]] = ahead[n]
    send_owner = jnp.where(odd, dp_index(ahead_odd), dp_index(ahead_yxz))
    send_ids = out_slot[send_owner * slot_share + slot_order % slot_share]
    return gathered_at, send_ids


def place_tiles(source, tiles, row_blocks, col_blocks, rows_per_step):
    tile_width = tiles.shape[-1]

    def kernel(source_ref, tiles_ref, out_ref):
        step = pl.program_id(0)
        for row in range(rows_per_step):
            for col in range(col_blocks):
                pick = source_ref[(step * rows_per_step + row) * col_blocks + col]
                tile = tiles_ref[jnp.maximum(pick, 0)]
                tile = jnp.where(pick >= 0, tile, jnp.zeros_like(tile))
                out_ref[
                    row * tile_width : (row + 1) * tile_width,
                    col * tile_width : (col + 1) * tile_width,
                ] = tile

    grid_spec = pltpu.PrefetchScalarGridSpec(
        num_scalar_prefetch=1,
        grid=(row_blocks // rows_per_step,),
        in_specs=[pl.BlockSpec(tiles.shape, lambda step, src: (0, 0, 0))],
        out_specs=pl.BlockSpec(
            (rows_per_step * tile_width, col_blocks * tile_width), lambda step, src: (step, 0)
        ),
    )
    return pl.pallas_call(
        kernel,
        grid_spec=grid_spec,
        out_shape=jax.ShapeDtypeStruct(
            (row_blocks * tile_width, col_blocks * tile_width), tiles.dtype
        ),
        interpret=INTERPRET,
    )(source, tiles)


def tile_products(tile_ids, left_t, right, col_blocks, slots_per_step):
    slot_count = tile_ids.shape[0]
    tile_width = left_t.shape[-2]

    def kernel(ids_ref, left_ref, right_ref, out_ref):
        step = pl.program_id(0)
        for slot in range(slots_per_step):
            tile = ids_ref[step * slots_per_step + slot]
            start = pl.multiple_of((tile % col_blocks) * tile_width, tile_width)
            out_ref[slot] = jnp.dot(
                left_ref[tile // col_blocks],
                right_ref[:, pl.ds(start, tile_width)],
                preferred_element_type=jnp.float32,
            ).astype(out_ref.dtype)

    grid_spec = pltpu.PrefetchScalarGridSpec(
        num_scalar_prefetch=1,
        grid=(slot_count // slots_per_step,),
        in_specs=[
            pl.BlockSpec(left_t.shape, lambda step, ids: (0, 0, 0)),
            pl.BlockSpec(right.shape, lambda step, ids: (0, 0)),
        ],
        out_specs=pl.BlockSpec(
            (slots_per_step, tile_width, tile_width), lambda step, ids: (step, 0, 0)
        ),
    )
    return pl.pallas_call(
        kernel,
        grid_spec=grid_spec,
        out_shape=jax.ShapeDtypeStruct((slot_count, tile_width, tile_width), jnp.bfloat16),
        interpret=INTERPRET,
    )(tile_ids, left_t, right)


def on_device(activations_in, cotangent, value_tiles, value_ids, out_tiles, out_ids, out_count):
    section_index = lax.axis_index("section")
    section_count = lax.axis_size("section")
    shard_count = lax.axis_size("dp")
    shard_index = lax.axis_index("dp")
    micro_count = activations_in.shape[0]
    tok_rows = activations_in.shape[1]
    model_width = activations_in.shape[2]
    all_rows = micro_count * tok_rows
    tile_width = value_tiles.shape[-1]
    value_width = VW
    value_blocks = value_width // tile_width
    model_blocks = model_width // tile_width
    slot_share = out_tiles.shape[1]
    out_slot = out_ids[0]
    live_mask = (jnp.arange(slot_share, dtype=jnp.int32)[None, :] < out_count[0][:, None]).reshape(
        -1
    )
    own_live = lax.dynamic_slice_in_dim(live_mask, shard_index * slot_share, slot_share)
    gathered = ring_gather(out_tiles[0], section_count, shard_count).reshape(
        -1, tile_width, tile_width
    )
    gathered_at, send_ids = slot_maps(section_index, shard_index, out_slot, slot_share)

    tile_numbers = jnp.arange(value_blocks * model_blocks, dtype=jnp.int32)
    value_order = jnp.arange(value_ids.shape[1], dtype=jnp.int32)
    value_source = jnp.max(
        jnp.where(value_ids[0][None, :] == tile_numbers[:, None], value_order[None, :], -1), axis=1
    )
    value_w = place_tiles(value_source, value_tiles[0], model_blocks, value_blocks, 8)
    out_source = (
        jnp.full((value_blocks * model_blocks,), -1, jnp.int32)
        .at[out_slot]
        .set(jnp.where(live_mask, gathered_at, -1), unique_indices=True)
    )
    out_w = place_tiles(out_source, gathered, value_blocks, model_blocks, 1)

    def forward_layer(hidden):
        value_rows = jnp.dot(hidden, value_w, preferred_element_type=jnp.float32).astype(
            jnp.bfloat16
        )
        update = jnp.dot(value_rows, out_w, preferred_element_type=jnp.float32)
        result = (hidden.astype(jnp.float32) + update).astype(jnp.bfloat16)
        return value_rows, result

    def backward_layer(grad_rows):
        grad_values = lax.dot_general(
            grad_rows, out_w, (((1,), (1,)), ((), ())), preferred_element_type=jnp.float32
        ).astype(jnp.bfloat16)
        grad_values = lax.optimization_barrier(grad_values)
        extra_term = lax.dot_general(
            grad_values, value_w, (((1,), (1,)), ((), ())), preferred_element_type=jnp.float32
        )
        return (grad_rows.astype(jnp.float32) + extra_term).astype(jnp.bfloat16)

    first_input = activations_in.reshape(all_rows, model_width)
    last_grad = cotangent.reshape(all_rows, model_width)
    value_store = jnp.zeros((all_rows, value_width), jnp.bfloat16)
    act_store = jnp.zeros((all_rows, model_width), jnp.bfloat16)
    input_store = jnp.zeros((all_rows, model_width), jnp.bfloat16)
    used_grad = jnp.zeros((all_rows, model_width), jnp.bfloat16)
    forward_in = first_input
    backward_in = last_grad
    for step_number in range(section_count):
        back_section = section_count - 1 - step_number
        value_store, act_store = lax.cond(
            section_index == step_number,
            lambda ops: forward_layer(ops[0]),
            lambda ops: (ops[1], ops[2]),
            (forward_in, value_store, act_store),
        )
        input_store, used_grad = lax.cond(
            section_index == back_section,
            lambda ops: (backward_layer(ops[0]), ops[0]),
            lambda ops: (ops[1], ops[2]),
            (backward_in, input_store, used_grad),
        )
        if step_number + 1 < section_count:
            outgoing = jnp.where(section_index == step_number, act_store, input_store)
            incoming = lax.ppermute(
                outgoing,
                "section",
                [(step_number, step_number + 1), (back_section, back_section - 1)],
            )
            forward_in = incoming
            backward_in = incoming

    grad_scale = 1.0 / math.sqrt(micro_count * tok_rows * shard_count)
    values_t = value_store.reshape(all_rows, value_blocks, tile_width).transpose(1, 2, 0)
    picked = tile_products(send_ids, values_t, used_grad, model_blocks, 96)
    summed = ring_reduce(
        picked.reshape(*DP_DIMS, slot_share, tile_width, tile_width), section_count, shard_count
    )
    scaled = summed * grad_scale
    out_grad = jnp.where(own_live[:, None, None], scaled, jnp.zeros_like(scaled))
    section_out = act_store.reshape(micro_count, tok_rows, model_width)
    grad_out = input_store.reshape(micro_count, tok_rows, model_width)
    return (section_out[None], grad_out[None], out_grad[None])


def solution(mesh):
    in_specs = (
        P(None, "dp", None),
        P(None, "dp", None),
        P("section", None, None, None),
        P("section", None),
        P("section", "dp", None, None),
        P("section", None),
        P("section", None),
    )
    out_specs = (
        P("section", None, "dp", None),
        P("section", None, "dp", None),
        P("section", "dp", None, None),
    )
    return jax.shard_map(
        on_device, mesh=mesh, in_specs=in_specs, out_specs=out_specs, check_vma=False
    )
```

```python
import math

import jax
import jax.numpy as jnp
from jax import lax
from jax.experimental import pallas as pl
from jax.experimental.pallas import tpu as pltpu
from jax.sharding import PartitionSpec as P

VW = 512
INTERPRET = False
DP_DIMS = (4, 4, 4)
STAGE_AXES = ((1, 0, 2), (0, 1, 2))


def dp_coords(index):
    return [index // (DP_DIMS[1] * DP_DIMS[2]), (index // DP_DIMS[2]) % DP_DIMS[1], index % DP_DIMS[2]]


def dp_index(coords):
    return (coords[0] * DP_DIMS[1] + coords[1]) * DP_DIMS[2] + coords[2]


def shift_pairs(stage, shift, section_count, shard_count):
    pairs = []
    for linear in range(section_count * shard_count):
        section, shard = divmod(linear, shard_count)
        coords = dp_coords(shard)
        axis = STAGE_AXES[section % 2][stage]
        coords[axis] = (coords[axis] + shift) % DP_DIMS[axis]
        pairs.append((linear, section * shard_count + dp_index(coords)))
    return pairs


def ring_reduce(parts, section_count, shard_count):
    for stage in range(3):
        width = DP_DIMS[STAGE_AXES[0][stage]]
        total = parts[0].astype(jnp.float32)
        for shift in range(1, width):
            total = total + lax.ppermute(
                parts[shift], ("section", "dp"), shift_pairs(stage, shift, section_count, shard_count)
            ).astype(jnp.float32)
        parts = total.astype(jnp.bfloat16) if stage < 2 else total
    return parts


def ring_gather(block, section_count, shard_count):
    for stage in reversed(range(3)):
        width = DP_DIMS[STAGE_AXES[0][stage]]
        pieces = [block] + [
            lax.ppermute(
                block, ("section", "dp"), shift_pairs(stage, shift, section_count, shard_count)
            )
            for shift in range(1, width)
        ]
        block = jnp.stack(pieces)
    return block


def slot_maps(section_index, shard_index, out_slot, slot_share):
    odd = section_index % 2 == 1
    mine = dp_coords(shard_index)
    own_axes = [jnp.where(odd, mine[STAGE_AXES[1][n]], mine[STAGE_AXES[0][n]]) for n in range(3)]
    slot_order = jnp.arange(out_slot.shape[0], dtype=jnp.int32)
    owner = dp_coords(slot_order // slot_share)
    owner_axes = [
        jnp.where(odd, owner[STAGE_AXES[1][n]], owner[STAGE_AXES[0][n]]) for n in range(3)
    ]
    behind = [(own_axes[n] - owner_axes[n]) % DP_DIMS[STAGE_AXES[0][n]] for n in range(3)]
    gathered_at = (
        ((behind[0] * DP_DIMS[STAGE_AXES[0][1]] + behind[1]) * DP_DIMS[STAGE_AXES[0][2]] + behind[2])
        * slot_share
        + slot_order % slot_share
    )
    ahead = [
        (own_axes[n] + (slot_order // slot_share) // math.prod(
            DP_DIMS[STAGE_AXES[0][m]] for m in range(n + 1, 3)
        ) % DP_DIMS[STAGE_AXES[0][n]]) % DP_DIMS[STAGE_AXES[0][n]]
        for n in range(3)
    ]
    ahead_yxz = [None, None, None]
    for n in range(3):
        ahead_yxz[STAGE_AXES[0][n]] = ahead[n]
    ahead_odd = [None, None, None]
    for n in range(3):
        ahead_odd[STAGE_AXES[1][n]] = ahead[n]
    send_owner = jnp.where(odd, dp_index(ahead_odd), dp_index(ahead_yxz))
    send_ids = out_slot[send_owner * slot_share + slot_order % slot_share]
    return gathered_at, send_ids


def place_tiles(source, tiles, row_blocks, col_blocks, rows_per_step):
    tile_width = tiles.shape[-1]

    def kernel(source_ref, tiles_ref, out_ref):
        step = pl.program_id(0)
        for row in range(rows_per_step):
            for col in range(col_blocks):
                pick = source_ref[(step * rows_per_step + row) * col_blocks + col]
                tile = tiles_ref[jnp.maximum(pick, 0)]
                tile = jnp.where(pick >= 0, tile, jnp.zeros_like(tile))
                out_ref[
                    row * tile_width : (row + 1) * tile_width,
                    col * tile_width : (col + 1) * tile_width,
                ] = tile

    grid_spec = pltpu.PrefetchScalarGridSpec(
        num_scalar_prefetch=1,
        grid=(row_blocks // rows_per_step,),
        in_specs=[pl.BlockSpec(tiles.shape, lambda step, src: (0, 0, 0))],
        out_specs=pl.BlockSpec(
            (rows_per_step * tile_width, col_blocks * tile_width), lambda step, src: (step, 0)
        ),
    )
    return pl.pallas_call(
        kernel,
        grid_spec=grid_spec,
        out_shape=jax.ShapeDtypeStruct(
            (row_blocks * tile_width, col_blocks * tile_width), tiles.dtype
        ),
        interpret=INTERPRET,
    )(source, tiles)


def tile_products(tile_ids, left_t, right, col_blocks, slots_per_step):
    slot_count = tile_ids.shape[0]
    tile_width = left_t.shape[-2]

    def kernel(ids_ref, left_ref, right_ref, out_ref):
        step = pl.program_id(0)
        for slot in range(slots_per_step):
            tile = ids_ref[step * slots_per_step + slot]
            start = pl.multiple_of((tile % col_blocks) * tile_width, tile_width)
            out_ref[slot] = jnp.dot(
                left_ref[tile // col_blocks],
                right_ref[:, pl.ds(start, tile_width)],
                preferred_element_type=jnp.float32,
            ).astype(out_ref.dtype)

    grid_spec = pltpu.PrefetchScalarGridSpec(
        num_scalar_prefetch=1,
        grid=(slot_count // slots_per_step,),
        in_specs=[
            pl.BlockSpec(left_t.shape, lambda step, ids: (0, 0, 0)),
            pl.BlockSpec(right.shape, lambda step, ids: (0, 0)),
        ],
        out_specs=pl.BlockSpec(
            (slots_per_step, tile_width, tile_width), lambda step, ids: (step, 0, 0)
        ),
    )
    return pl.pallas_call(
        kernel,
        grid_spec=grid_spec,
        out_shape=jax.ShapeDtypeStruct((slot_count, tile_width, tile_width), jnp.bfloat16),
        interpret=INTERPRET,
    )(tile_ids, left_t, right)


def on_device(activations_in, cotangent, value_tiles, value_ids, out_tiles, out_ids, out_count):
    section_index = lax.axis_index("section")
    section_count = lax.axis_size("section")
    shard_count = lax.axis_size("dp")
    shard_index = lax.axis_index("dp")
    micro_count = activations_in.shape[0]
    tok_rows = activations_in.shape[1]
    model_width = activations_in.shape[2]
    all_rows = micro_count * tok_rows
    tile_width = value_tiles.shape[-1]
    value_width = VW
    value_blocks = value_width // tile_width
    model_blocks = model_width // tile_width
    slot_share = out_tiles.shape[1]
    out_slot = out_ids[0]
    live_mask = (jnp.arange(slot_share, dtype=jnp.int32)[None, :] < out_count[0][:, None]).reshape(
        -1
    )
    own_live = lax.dynamic_slice_in_dim(live_mask, shard_index * slot_share, slot_share)
    gathered = ring_gather(out_tiles[0], section_count, shard_count).reshape(
        -1, tile_width, tile_width
    )
    gathered_at, send_ids = slot_maps(section_index, shard_index, out_slot, slot_share)

    tile_numbers = jnp.arange(value_blocks * model_blocks, dtype=jnp.int32)
    value_order = jnp.arange(value_ids.shape[1], dtype=jnp.int32)
    value_source = jnp.max(
        jnp.where(value_ids[0][None, :] == tile_numbers[:, None], value_order[None, :], -1), axis=1
    )
    value_w = place_tiles(value_source, value_tiles[0], model_blocks, value_blocks, 8)
    out_source = (
        jnp.full((value_blocks * model_blocks,), -1, jnp.int32)
        .at[out_slot]
        .set(jnp.where(live_mask, gathered_at, -1), unique_indices=True)
    )
    out_w = place_tiles(out_source, gathered, value_blocks, model_blocks, 2)

    def forward_layer(hidden):
        value_rows = jnp.dot(hidden, value_w, preferred_element_type=jnp.float32).astype(
            jnp.bfloat16
        )
        update = jnp.dot(value_rows, out_w, preferred_element_type=jnp.float32)
        result = (hidden.astype(jnp.float32) + update).astype(jnp.bfloat16)
        return value_rows, result

    def backward_layer(grad_rows):
        grad_values = lax.dot_general(
            grad_rows, out_w, (((1,), (1,)), ((), ())), preferred_element_type=jnp.float32
        ).astype(jnp.bfloat16)
        grad_values = lax.optimization_barrier(grad_values)
        extra_term = lax.dot_general(
            grad_values, value_w, (((1,), (1,)), ((), ())), preferred_element_type=jnp.float32
        )
        return (grad_rows.astype(jnp.float32) + extra_term).astype(jnp.bfloat16)

    first_input = activations_in.reshape(all_rows, model_width)
    last_grad = cotangent.reshape(all_rows, model_width)
    value_store = jnp.zeros((all_rows, value_width), jnp.bfloat16)
    act_store = jnp.zeros((all_rows, model_width), jnp.bfloat16)
    input_store = jnp.zeros((all_rows, model_width), jnp.bfloat16)
    used_grad = jnp.zeros((all_rows, model_width), jnp.bfloat16)
    forward_in = first_input
    backward_in = last_grad
    for step_number in range(section_count):
        back_section = section_count - 1 - step_number
        value_store, act_store = lax.cond(
            section_index == step_number,
            lambda ops: forward_layer(ops[0]),
            lambda ops: (ops[1], ops[2]),
            (forward_in, value_store, act_store),
        )
        input_store, used_grad = lax.cond(
            section_index == back_section,
            lambda ops: (backward_layer(ops[0]), ops[0]),
            lambda ops: (ops[1], ops[2]),
            (backward_in, input_store, used_grad),
        )
        if step_number + 1 < section_count:
            outgoing = jnp.where(section_index == step_number, act_store, input_store)
            incoming = lax.ppermute(
                outgoing,
                "section",
                [(step_number, step_number + 1), (back_section, back_section - 1)],
            )
            forward_in = incoming
            backward_in = incoming

    grad_scale = 1.0 / math.sqrt(micro_count * tok_rows * shard_count)
    values_t = value_store.reshape(all_rows, value_blocks, tile_width).transpose(1, 2, 0)
    picked = tile_products(send_ids, values_t, used_grad, model_blocks, 96)
    summed = ring_reduce(
        picked.reshape(*DP_DIMS, slot_share, tile_width, tile_width), section_count, shard_count
    )
    scaled = summed * grad_scale
    out_grad = jnp.where(own_live[:, None, None], scaled, jnp.zeros_like(scaled))
    section_out = act_store.reshape(micro_count, tok_rows, model_width)
    grad_out = input_store.reshape(micro_count, tok_rows, model_width)
    return (section_out[None], grad_out[None], out_grad[None])


def solution(mesh):
    in_specs = (
        P(None, "dp", None),
        P(None, "dp", None),
        P("section", None, None, None),
        P("section", None),
        P("section", "dp", None, None),
        P("section", None),
        P("section", None),
    )
    out_specs = (
        P("section", None, "dp", None),
        P("section", None, "dp", None),
        P("section", "dp", None, None),
    )
    return jax.shard_map(
        on_device, mesh=mesh, in_specs=in_specs, out_specs=out_specs, check_vma=False
    )
```

```python
import math

import jax
import jax.numpy as jnp
from jax import lax
from jax.experimental import pallas as pl
from jax.experimental.pallas import tpu as pltpu
from jax.sharding import PartitionSpec as P

VW = 512
INTERPRET = False
DP_DIMS = (4, 4, 4)
STAGE_AXES = ((1, 0, 2), (0, 1, 2))


def dp_coords(index):
    return [index // (DP_DIMS[1] * DP_DIMS[2]), (index // DP_DIMS[2]) % DP_DIMS[1], index % DP_DIMS[2]]


def dp_index(coords):
    return (coords[0] * DP_DIMS[1] + coords[1]) * DP_DIMS[2] + coords[2]


def shift_pairs(stage, shift, section_count, shard_count):
    pairs = []
    for linear in range(section_count * shard_count):
        section, shard = divmod(linear, shard_count)
        coords = dp_coords(shard)
        axis = STAGE_AXES[section % 2][stage]
        coords[axis] = (coords[axis] + shift) % DP_DIMS[axis]
        pairs.append((linear, section * shard_count + dp_index(coords)))
    return pairs


def ring_reduce(parts, section_count, shard_count):
    for stage in range(3):
        width = DP_DIMS[STAGE_AXES[0][stage]]
        total = parts[0].astype(jnp.float32)
        for shift in range(1, width):
            total = total + lax.ppermute(
                parts[shift], ("section", "dp"), shift_pairs(stage, shift, section_count, shard_count)
            ).astype(jnp.float32)
        parts = total.astype(jnp.bfloat16) if stage < 2 else total
    return parts


def ring_gather(block, section_count, shard_count):
    for stage in reversed(range(3)):
        width = DP_DIMS[STAGE_AXES[0][stage]]
        pieces = [block] + [
            lax.ppermute(
                block, ("section", "dp"), shift_pairs(stage, shift, section_count, shard_count)
            )
            for shift in range(1, width)
        ]
        block = jnp.stack(pieces)
    return block


def slot_maps(section_index, shard_index, out_slot, slot_share):
    odd = section_index % 2 == 1
    mine = dp_coords(shard_index)
    own_axes = [jnp.where(odd, mine[STAGE_AXES[1][n]], mine[STAGE_AXES[0][n]]) for n in range(3)]
    slot_order = jnp.arange(out_slot.shape[0], dtype=jnp.int32)
    owner = dp_coords(slot_order // slot_share)
    owner_axes = [
        jnp.where(odd, owner[STAGE_AXES[1][n]], owner[STAGE_AXES[0][n]]) for n in range(3)
    ]
    behind = [(own_axes[n] - owner_axes[n]) % DP_DIMS[STAGE_AXES[0][n]] for n in range(3)]
    gathered_at = (
        ((behind[0] * DP_DIMS[STAGE_AXES[0][1]] + behind[1]) * DP_DIMS[STAGE_AXES[0][2]] + behind[2])
        * slot_share
        + slot_order % slot_share
    )
    ahead = [
        (own_axes[n] + (slot_order // slot_share) // math.prod(
            DP_DIMS[STAGE_AXES[0][m]] for m in range(n + 1, 3)
        ) % DP_DIMS[STAGE_AXES[0][n]]) % DP_DIMS[STAGE_AXES[0][n]]
        for n in range(3)
    ]
    ahead_yxz = [None, None, None]
    for n in range(3):
        ahead_yxz[STAGE_AXES[0][n]] = ahead[n]
    ahead_odd = [None, None, None]
    for n in range(3):
        ahead_odd[STAGE_AXES[1][n]] = ahead[n]
    send_owner = jnp.where(odd, dp_index(ahead_odd), dp_index(ahead_yxz))
    send_ids = out_slot[send_owner * slot_share + slot_order % slot_share]
    return gathered_at, send_ids


def place_tiles(source, tiles, row_blocks, col_blocks, rows_per_step):
    tile_width = tiles.shape[-1]

    def kernel(source_ref, tiles_ref, out_ref):
        step = pl.program_id(0)
        for row in range(rows_per_step):
            for col in range(col_blocks):
                pick = source_ref[(step * rows_per_step + row) * col_blocks + col]
                tile = tiles_ref[jnp.maximum(pick, 0)]
                tile = jnp.where(pick >= 0, tile, jnp.zeros_like(tile))
                out_ref[
                    row * tile_width : (row + 1) * tile_width,
                    col * tile_width : (col + 1) * tile_width,
                ] = tile

    grid_spec = pltpu.PrefetchScalarGridSpec(
        num_scalar_prefetch=1,
        grid=(row_blocks // rows_per_step,),
        in_specs=[pl.BlockSpec(tiles.shape, lambda step, src: (0, 0, 0))],
        out_specs=pl.BlockSpec(
            (rows_per_step * tile_width, col_blocks * tile_width), lambda step, src: (step, 0)
        ),
    )
    return pl.pallas_call(
        kernel,
        grid_spec=grid_spec,
        out_shape=jax.ShapeDtypeStruct(
            (row_blocks * tile_width, col_blocks * tile_width), tiles.dtype
        ),
        interpret=INTERPRET,
    )(source, tiles)


def tile_products(tile_ids, left_t, right, col_blocks, slots_per_step):
    slot_count = tile_ids.shape[0]
    tile_width = left_t.shape[-2]

    def kernel(ids_ref, left_ref, right_ref, out_ref):
        step = pl.program_id(0)
        for slot in range(slots_per_step):
            tile = ids_ref[step * slots_per_step + slot]
            start = pl.multiple_of((tile % col_blocks) * tile_width, tile_width)
            out_ref[slot] = jnp.dot(
                left_ref[tile // col_blocks],
                right_ref[:, pl.ds(start, tile_width)],
                preferred_element_type=jnp.float32,
            ).astype(out_ref.dtype)

    grid_spec = pltpu.PrefetchScalarGridSpec(
        num_scalar_prefetch=1,
        grid=(slot_count // slots_per_step,),
        in_specs=[
            pl.BlockSpec(left_t.shape, lambda step, ids: (0, 0, 0)),
            pl.BlockSpec(right.shape, lambda step, ids: (0, 0)),
        ],
        out_specs=pl.BlockSpec(
            (slots_per_step, tile_width, tile_width), lambda step, ids: (step, 0, 0)
        ),
    )
    return pl.pallas_call(
        kernel,
        grid_spec=grid_spec,
        out_shape=jax.ShapeDtypeStruct((slot_count, tile_width, tile_width), jnp.bfloat16),
        interpret=INTERPRET,
    )(tile_ids, left_t, right)


def on_device(activations_in, cotangent, value_tiles, value_ids, out_tiles, out_ids, out_count):
    section_index = lax.axis_index("section")
    section_count = lax.axis_size("section")
    shard_count = lax.axis_size("dp")
    shard_index = lax.axis_index("dp")
    micro_count = activations_in.shape[0]
    tok_rows = activations_in.shape[1]
    model_width = activations_in.shape[2]
    all_rows = micro_count * tok_rows
    tile_width = value_tiles.shape[-1]
    value_width = VW
    value_blocks = value_width // tile_width
    model_blocks = model_width // tile_width
    slot_share = out_tiles.shape[1]
    out_slot = out_ids[0]
    live_mask = (jnp.arange(slot_share, dtype=jnp.int32)[None, :] < out_count[0][:, None]).reshape(
        -1
    )
    own_live = lax.dynamic_slice_in_dim(live_mask, shard_index * slot_share, slot_share)
    gathered = ring_gather(out_tiles[0], section_count, shard_count).reshape(
        -1, tile_width, tile_width
    )
    gathered_at, send_ids = slot_maps(section_index, shard_index, out_slot, slot_share)

    tile_numbers = jnp.arange(value_blocks * model_blocks, dtype=jnp.int32)
    value_order = jnp.arange(value_ids.shape[1], dtype=jnp.int32)
    value_source = jnp.max(
        jnp.where(value_ids[0][None, :] == tile_numbers[:, None], value_order[None, :], -1), axis=1
    )
    value_w = place_tiles(value_source, value_tiles[0], model_blocks, value_blocks, 8)
    out_source = (
        jnp.full((value_blocks * model_blocks,), -1, jnp.int32)
        .at[out_slot]
        .set(jnp.where(live_mask, gathered_at, -1), unique_indices=True)
    )
    out_w = place_tiles(out_source, gathered, value_blocks, model_blocks, 2)

    def forward_layer(hidden):
        value_rows = jnp.dot(hidden, value_w, preferred_element_type=jnp.float32).astype(
            jnp.bfloat16
        )
        update = jnp.dot(value_rows, out_w, preferred_element_type=jnp.float32)
        result = (hidden.astype(jnp.float32) + update).astype(jnp.bfloat16)
        return value_rows, result

    def backward_layer(grad_rows):
        grad_values = lax.dot_general(
            grad_rows, out_w, (((1,), (1,)), ((), ())), preferred_element_type=jnp.float32
        ).astype(jnp.bfloat16)
        grad_values = lax.optimization_barrier(grad_values)
        extra_term = lax.dot_general(
            grad_values, value_w, (((1,), (1,)), ((), ())), preferred_element_type=jnp.float32
        )
        return (grad_rows.astype(jnp.float32) + extra_term).astype(jnp.bfloat16)

    first_input = activations_in.reshape(all_rows, model_width)
    last_grad = cotangent.reshape(all_rows, model_width)
    value_store = jnp.zeros((all_rows, value_width), jnp.bfloat16)
    act_store = jnp.zeros((all_rows, model_width), jnp.bfloat16)
    input_store = jnp.zeros((all_rows, model_width), jnp.bfloat16)
    used_grad = jnp.zeros((all_rows, model_width), jnp.bfloat16)
    forward_in = first_input
    backward_in = last_grad
    for step_number in range(section_count):
        back_section = section_count - 1 - step_number
        value_store, act_store = lax.cond(
            section_index == step_number,
            lambda ops: forward_layer(ops[0]),
            lambda ops: (ops[1], ops[2]),
            (forward_in, value_store, act_store),
        )
        input_store, used_grad = lax.cond(
            section_index == back_section,
            lambda ops: (backward_layer(ops[0]), ops[0]),
            lambda ops: (ops[1], ops[2]),
            (backward_in, input_store, used_grad),
        )
        if step_number + 1 < section_count:
            outgoing = jnp.where(section_index == step_number, act_store, input_store)
            incoming = lax.ppermute(
                outgoing,
                "section",
                [(step_number, step_number + 1), (back_section, back_section - 1)],
            )
            forward_in = incoming
            backward_in = incoming

    grad_scale = 1.0 / math.sqrt(micro_count * tok_rows * shard_count)
    values_t = value_store.reshape(all_rows, value_blocks, tile_width).transpose(1, 2, 0)
    picked = tile_products(send_ids, values_t, used_grad, model_blocks, 192)
    summed = ring_reduce(
        picked.reshape(*DP_DIMS, slot_share, tile_width, tile_width), section_count, shard_count
    )
    scaled = summed * grad_scale
    out_grad = jnp.where(own_live[:, None, None], scaled, jnp.zeros_like(scaled))
    section_out = act_store.reshape(micro_count, tok_rows, model_width)
    grad_out = input_store.reshape(micro_count, tok_rows, model_width)
    return (section_out[None], grad_out[None], out_grad[None])


def solution(mesh):
    in_specs = (
        P(None, "dp", None),
        P(None, "dp", None),
        P("section", None, None, None),
        P("section", None),
        P("section", "dp", None, None),
        P("section", None),
        P("section", None),
    )
    out_specs = (
        P("section", None, "dp", None),
        P("section", None, "dp", None),
        P("section", "dp", None, None),
    )
    return jax.shard_map(
        on_device, mesh=mesh, in_specs=in_specs, out_specs=out_specs, check_vma=False
    )
```
